128 devices in a mesh: pb: 8 (over z, y_lo), kv: 16 (over x, y_hi, core).
Axes of the slice: x: 4, y: 4 (y_hi: 2, y_lo: 2; y = y_hi * 2 + y_lo), z: 4, core: 2. Of those that a mesh axis runs over, the one named last changes fastest.
Arguments:
- slab_start: int32 [1], replicated, may hold values from 0 to 12288
- queries: bfloat16 [4096, 4096], P('pb', 'kv'), may hold values from -6 to 6
- keys: bfloat16 [16384, 2048], P('kv'), may hold values from -6 to 6
- values: bfloat16 [16384, 2048], P('kv'), may hold values from -6 to 6
- out_weight: bfloat16 [4096, 4608], P('kv'), may hold values from -0.09375 to 0.09375
Outputs:
- projected: float32 [4096, 4608], P(('pb', 'kv'))
The draws below stay inside these ranges and needn't reach their ends.
Inputs may be any that keep to these rules, and one draw needn't show every extreme that they name: The slab lies inside the context: slab_start + 4096 <= 16384.
All inputs are finite; a program needn't handle non-finite values.
Results may differ from the reference program's by a relative error of at most 0.01.
Values may be sent and summed in bfloat16 or wider, within the bound.
No kernel may reach another device: no remote copies, remote signals or barrier semaphores. Data moves between devices by JAX's collectives and lax.ppermute only.
A program may use at most 128 MiB of HBM per device.

```python
import jax
import jax.numpy as jnp
from jax import lax

D = 4608
HQ = 32
KVH = 16
HD = 128
CAP = 50
SCALAR = 144
SQ = 4096
CTX = 16384


def block_levels(stream_key, dims, cuts, smallest, high):
    loudness, own = 1.0, jax.random.fold_in(stream_key, 6)
    for position, parts in cuts:
        heights = jnp.exp(jax.random.uniform(jax.random.fold_in(own, position), (parts,), jnp.float32, smallest / len(cuts), high / len(cuts)))
        loudness = loudness * jnp.repeat(heights, dims[position] // parts).reshape([-1 if axis == position else 1 for axis in range(len(dims))])
    return loudness


def centred(rng, dims, scale, limit, cuts=(), kind=jnp.bfloat16):
    values = jax.random.normal(rng, dims, jnp.float32) * scale
    if len(cuts) > 0:
        values = block_levels(rng, dims, cuts, -0.22, 0.18) * values
    return jnp.clip(values, min=-limit, max=limit).astype(kind)


def setup_inputs(seed: int = 0) -> dict:
    key_of = jax.random.split(jax.random.key(seed), 6)
    slab_start = jax.random.randint(key_of[0], (1,), 0, CTX - SQ + 1).astype(jnp.int32)
    queries = centred(key_of[1], (SQ, HQ * HD), 1.0, 6.0, ((0, 8), (1, 16)))
    keys = centred(key_of[2], (CTX, KVH * HD), 1.0, 6.0, ((0, 16),))
    values = centred(key_of[3], (CTX, KVH * HD), 1.0, 6.0, ((0, 16),))
    out_weight = centred(key_of[4], (HQ * HD, D), (HQ * HD) ** -0.5, 0.09375, ((0, 16),))
    return {"slab_start": slab_start, "queries": queries, "keys": keys, "values": values, "out_weight": out_weight}


def capped(raw):
    return CAP * jnp.tanh(raw / CAP)


def reference(slab_start, queries, keys, values, out_weight):
    group = HQ // KVH
    first = slab_start[0]
    scale = SCALAR ** -0.5
    key_pos = jnp.arange(CTX, dtype=jnp.int32)
    tile = min(512, SQ)
    tiles = SQ // tile
    q_tiles = queries.reshape(tiles, tile, KVH, group, HD)
    key_heads = keys.reshape(CTX, KVH, HD)
    value_heads = values.reshape(CTX, KVH, HD)

    def one_head(head):
        key_one = lax.dynamic_index_in_dim(key_heads, head, 1, keepdims=False)
        value_one = lax.dynamic_index_in_dim(value_heads, head, 1, keepdims=False)

        def one_tile(index):
            block = lax.dynamic_index_in_dim(q_tiles, index, 0, keepdims=False)
            block = lax.dynamic_index_in_dim(block, head, 1, keepdims=False)
            block = block.reshape(tile * group, HD)
            rows = jnp.arange(tile * group, dtype=jnp.int32) // group
            positions = first + index * tile + rows
            raw = jnp.dot(block, key_one.T, preferred_element_type=jnp.float32) * scale
            scores = capped(raw)
            kept = key_pos[None, :] <= positions[:, None]
            scores = jnp.where(kept, scores, -1e30)
            top = jnp.max(scores, axis=1, keepdims=True)
            prob = jnp.where(kept, jnp.exp(scores - top), 0.0)
            total = jnp.sum(prob, axis=1, keepdims=True)
            summed = jnp.dot(prob.astype(jnp.bfloat16), value_one, preferred_element_type=jnp.float32)
            mixed = (summed / total).astype(jnp.bfloat16)
            return mixed.reshape(tile, group * HD)

        return lax.map(one_tile, jnp.arange(tiles, dtype=jnp.int32))

    per_head = lax.map(one_head, jnp.arange(KVH, dtype=jnp.int32))
    attended = per_head.transpose(1, 2, 0, 3).reshape(SQ, HQ * HD)
    return jnp.dot(attended, out_weight, preferred_element_type=jnp.float32)
```

```python
import jax
import jax.numpy as jnp
from jax import lax
from jax.sharding import Mesh, PartitionSpec as P

HQ = 32
KVH = 16
HD = 128
CAP = 50
SCALAR = 144
KV = ("kx", "kc")


def attend_block(carry, q_block, q_pos, key_part, value_part, key_pos):
    top, total, summed = carry
    raw = jnp.einsum("gqd,kgd->gqk", q_block, key_part, preferred_element_type=jnp.float32)
    scores = CAP * jnp.tanh(raw * SCALAR ** (-0.5) / CAP)
    kept = key_pos[None, None, :] <= q_pos[None, :, None]
    scores = jnp.where(kept, scores, -1e30)
    new_top = jnp.maximum(top, jnp.max(scores, axis=2))
    keep = jnp.exp(top - new_top)
    prob = jnp.where(kept, jnp.exp(scores - new_top[:, :, None]), 0.0)
    total = total * keep + jnp.sum(prob, axis=2)
    weights = prob.astype(jnp.bfloat16)
    summed = summed * keep[:, :, None] + jnp.einsum(
        "gqk,kgd->gqd", weights, value_part, preferred_element_type=jnp.float32
    )
    return (new_top, total, summed)


def empty_state(heads, rows):
    return (
        jnp.full((heads, rows), -1e30, jnp.float32),
        jnp.zeros((heads, rows), jnp.float32),
        jnp.zeros((heads, rows, HD), jnp.float32),
    )


def by_heads(queries, keys, values, positions):
    n_kv = lax.axis_size(KV)
    group = HQ // KVH
    rows_dev = queries.shape[0]
    key_dev = keys.shape[0]
    kv_feat = keys.shape[1] // n_kv
    pair = jnp.stack(
        (keys.reshape(key_dev, n_kv, kv_feat), values.reshape(key_dev, n_kv, kv_feat)), axis=0
    ).transpose(2, 0, 1, 3)
    both = lax.all_to_all(pair, KV, split_axis=0, concat_axis=0, tiled=True)
    key_all = both[:, 0].reshape(n_kv * key_dev, kv_feat // HD, HD)
    value_all = both[:, 1].reshape(n_kv * key_dev, kv_feat // HD, HD)
    context = key_all.shape[0]
    kv_local = kv_feat // HD
    tile = min(256, rows_dev)
    tiles = rows_dev // tile
    width = min(2048, context)
    q_tiles = queries.reshape(tiles, tile, kv_local, group, HD)
    p_tiles = positions.reshape(tiles, tile)

    def one_tile(item):
        q_block, pos = item
        q_block = q_block.transpose(1, 0, 2, 3).reshape(kv_local, tile * group, HD)
        q_pos = jnp.repeat(pos, group)
        count = jnp.max(pos) // width + 1

        def step(index, carry):
            key_part = lax.dynamic_slice_in_dim(key_all, index * width, width, 0)
            value_part = lax.dynamic_slice_in_dim(value_all, index * width, width, 0)
            key_pos = index * width + jnp.arange(width, dtype=jnp.int32)
            return attend_block(carry, q_block, q_pos, key_part, value_part, key_pos)

        top, total, summed = lax.fori_loop(0, count, step, empty_state(kv_local, tile * group))
        mixed = (summed / total[:, :, None]).astype(jnp.bfloat16)
        return (
            mixed.reshape(kv_local, tile, group, HD)
            .transpose(1, 0, 2, 3)
            .reshape(tile, kv_local * group * HD)
        )

    result = lax.map(one_tile, (q_tiles, p_tiles))
    return result.reshape(rows_dev, kv_local * group * HD)


def per_device(slab_start, queries, keys, values, out_weight):
    rows_dev = queries.shape[0]
    first = slab_start[0]
    row_index = jnp.arange(rows_dev, dtype=jnp.int32)
    anchor = lax.axis_index("pb") * rows_dev + row_index
    positions = first + anchor
    attended = by_heads(queries, keys, values, positions)
    partial = jnp.dot(attended, out_weight, preferred_element_type=jnp.float32)
    n_chip = lax.axis_size("kx")
    n_core = lax.axis_size("kc")
    partial = partial.reshape(n_chip, n_core, rows_dev // (n_chip * n_core), partial.shape[1])
    core = lax.axis_index("kc")
    mine = lax.dynamic_index_in_dim(partial, core, 1, keepdims=False)
    theirs = lax.dynamic_index_in_dim(partial, 1 - core, 1, keepdims=False)
    on_chip = mine + lax.ppermute(theirs, "kc", [(0, 1), (1, 0)])
    parts = lax.all_to_all(
        on_chip.astype(jnp.bfloat16), "kx", split_axis=0, concat_axis=0, tiled=True
    )
    return jnp.sum(parts.astype(jnp.float32), axis=0)


def solution(mesh):
    n_pb, n_kv = mesh.devices.shape
    split = Mesh(mesh.devices.reshape(n_pb, n_kv // 2, 2), ("pb", "kx", "kc"))
    in_specs = (P(), P("pb", KV), P(KV, None), P(KV, None), P(KV, None))
    out_specs = P(("pb",) + KV, None)
    return jax.shard_map(
        per_device, mesh=split, in_specs=in_specs, out_specs=out_specs, check_vma=False
    )
```

```python
import jax
import jax.numpy as jnp
from jax import lax
from jax.sharding import Mesh, PartitionSpec as P

HQ = 32
KVH = 16
HD = 128
CAP = 50
SCALAR = 144
KV = ("kx", "kc")


def attend_block(carry, q_block, q_pos, key_part, value_part, key_pos):
    top, total, summed = carry
    raw = jnp.einsum("gqd,kgd->gqk", q_block, key_part, preferred_element_type=jnp.float32)
    scores = CAP * jnp.tanh(raw * SCALAR ** (-0.5) / CAP)
    kept = key_pos[None, None, :] <= q_pos[None, :, None]
    scores = jnp.where(kept, scores, -1e30)
    new_top = jnp.maximum(top, jnp.max(scores, axis=2))
    keep = jnp.exp(top - new_top)
    prob = jnp.where(kept, jnp.exp(scores - new_top[:, :, None]), 0.0)
    total = total * keep + jnp.sum(prob, axis=2)
    weights = prob.astype(jnp.bfloat16)
    summed = summed * keep[:, :, None] + jnp.einsum(
        "gqk,kgd->gqd", weights, value_part, preferred_element_type=jnp.float32
    )
    return (new_top, total, summed)


def empty_state(heads, rows):
    return (
        jnp.full((heads, rows), -1e30, jnp.float32),
        jnp.zeros((heads, rows), jnp.float32),
        jnp.zeros((heads, rows, HD), jnp.float32),
    )


def by_heads(queries, keys, values, positions, max_pos):
    n_kv = lax.axis_size(KV)
    me = lax.axis_index(KV)
    group = HQ // KVH
    rows_dev = queries.shape[0]
    key_dev = keys.shape[0]
    kv_local = keys.shape[1] // (n_kv * HD)
    kv_feat = kv_local * HD
    q_block = (
        queries.reshape(rows_dev, kv_local, group, HD)
        .transpose(1, 0, 2, 3)
        .reshape(kv_local, rows_dev * group, HD)
    )
    q_pos = jnp.repeat(positions, group)
    state = empty_state(kv_local, rows_dev * group)
    for shift in range(n_kv):
        dest = (me + shift) % n_kv
        src = (me - shift) % n_kv
        block = jnp.stack(
            (
                lax.dynamic_slice_in_dim(keys, dest * kv_feat, kv_feat, 1),
                lax.dynamic_slice_in_dim(values, dest * kv_feat, kv_feat, 1),
            ),
            axis=0,
        )
        if shift:
            block = lax.ppermute(block, KV, [(j, (j + shift) % n_kv) for j in range(n_kv)])
        block = block.reshape(2, key_dev, kv_local, HD)
        key_pos = src * key_dev + jnp.arange(key_dev, dtype=jnp.int32)

        def attend(carry, block=block, key_pos=key_pos):
            return attend_block(carry, q_block, q_pos, block[0], block[1], key_pos)

        state = lax.cond(src * key_dev <= max_pos, attend, lambda carry: carry, state)
    top, total, summed = state
    mixed = (summed / total[:, :, None]).astype(jnp.bfloat16)
    return (
        mixed.reshape(kv_local, rows_dev, group, HD)
        .transpose(1, 0, 2, 3)
        .reshape(rows_dev, kv_local * group * HD)
    )


def per_device(slab_start, queries, keys, values, out_weight):
    rows_dev = queries.shape[0]
    first = slab_start[0]
    row_index = jnp.arange(rows_dev, dtype=jnp.int32)
    anchor = lax.axis_index("pb") * rows_dev + row_index
    positions = first + anchor
    max_pos = first + (lax.axis_index("pb") + 1) * rows_dev - 1
    attended = by_heads(queries, keys, values, positions, max_pos)
    partial = jnp.dot(attended, out_weight, preferred_element_type=jnp.float32)
    n_chip = lax.axis_size("kx")
    n_core = lax.axis_size("kc")
    partial = partial.reshape(n_chip, n_core, rows_dev // (n_chip * n_core), partial.shape[1])
    core = lax.axis_index("kc")
    mine = lax.dynamic_index_in_dim(partial, core, 1, keepdims=False)
    theirs = lax.dynamic_index_in_dim(partial, 1 - core, 1, keepdims=False)
    on_chip = mine + lax.ppermute(theirs, "kc", [(0, 1), (1, 0)])
    parts = lax.all_to_all(
        on_chip.astype(jnp.bfloat16), "kx", split_axis=0, concat_axis=0, tiled=True
    )
    return jnp.sum(parts.astype(jnp.float32), axis=0)


def solution(mesh):
    n_pb, n_kv = mesh.devices.shape
    split = Mesh(mesh.devices.reshape(n_pb, n_kv // 2, 2), ("pb", "kx", "kc"))
    in_specs = (P(), P("pb", KV), P(KV, None), P(KV, None), P(KV, None))
    out_specs = P(("pb",) + KV, None)
    return jax.shard_map(
        per_device, mesh=split, in_specs=in_specs, out_specs=out_specs, check_vma=False
    )
```

```python
import jax
import jax.numpy as jnp
from jax import lax
from jax.sharding import Mesh, PartitionSpec as P

HQ = 32
KVH = 16
HD = 128
CAP = 50
SCALAR = 144
KV = ("kx", "kc")
LAG = 4


def attend_block(carry, q_block, q_pos, key_part, value_part, key_pos):
    top, total, summed = carry
    raw = jnp.einsum("gqd,kgd->gqk", q_block, key_part, preferred_element_type=jnp.float32)
    scores = CAP * jnp.tanh(raw * SCALAR ** (-0.5) / CAP)
    kept = key_pos[None, None, :] <= q_pos[None, :, None]
    scores = jnp.where(kept, scores, -1e30)
    new_top = jnp.maximum(top, jnp.max(scores, axis=2))
    keep = jnp.exp(top - new_top)
    prob = jnp.where(kept, jnp.exp(scores - new_top[:, :, None]), 0.0)
    total = total * keep + jnp.sum(prob, axis=2)
    weights = prob.astype(jnp.bfloat16)
    summed = summed * keep[:, :, None] + jnp.einsum(
        "gqk,kgd->gqd", weights, value_part, preferred_element_type=jnp.float32
    )
    return (new_top, total, summed)


def empty_state(heads, rows):
    return (
        jnp.full((heads, rows), -1e30, jnp.float32),
        jnp.zeros((heads, rows), jnp.float32),
        jnp.zeros((heads, rows, HD), jnp.float32),
    )


def by_heads(queries, keys, values, positions, max_pos):
    n_kv = lax.axis_size(KV)
    me = lax.axis_index(KV)
    group = HQ // KVH
    rows_dev = queries.shape[0]
    key_dev = keys.shape[0]
    kv_local = keys.shape[1] // (n_kv * HD)
    kv_feat = kv_local * HD
    q_block = (
        queries.reshape(rows_dev, kv_local, group, HD)
        .transpose(1, 0, 2, 3)
        .reshape(kv_local, rows_dev * group, HD)
    )
    q_pos = jnp.repeat(positions, group)
    state = empty_state(kv_local, rows_dev * group)
    sends = []
    for shift in range(n_kv):
        dest = (me + shift) % n_kv
        sends.append(
            jnp.stack(
                (
                    lax.dynamic_slice_in_dim(keys, dest * kv_feat, kv_feat, 1),
                    lax.dynamic_slice_in_dim(values, dest * kv_feat, kv_feat, 1),
                ),
                axis=0,
            )
        )
    received = [sends[0]]
    for shift in range(1, min(LAG + 1, n_kv)):
        received.append(lax.ppermute(sends[shift], KV, [(j, (j + shift) % n_kv) for j in range(n_kv)]))
    for shift in range(n_kv):
        src = (me - shift) % n_kv
        block = received[shift].reshape(2, key_dev, kv_local, HD)
        key_pos = src * key_dev + jnp.arange(key_dev, dtype=jnp.int32)

        def attend(carry, block=block, key_pos=key_pos):
            return attend_block(carry, q_block, q_pos, block[0], block[1], key_pos)

        state = lax.cond(src * key_dev <= max_pos, attend, lambda carry: carry, state)
        nxt = shift + LAG + 1
        if nxt < n_kv:
            payload, state = lax.optimization_barrier((sends[nxt], state))
            received.append(lax.ppermute(payload, KV, [(j, (j + nxt) % n_kv) for j in range(n_kv)]))
    top, total, summed = state
    mixed = (summed / total[:, :, None]).astype(jnp.bfloat16)
    return (
        mixed.reshape(kv_local, rows_dev, group, HD)
        .transpose(1, 0, 2, 3)
        .reshape(rows_dev, kv_local * group * HD)
    )


def per_device(slab_start, queries, keys, values, out_weight):
    rows_dev = queries.shape[0]
    first = slab_start[0]
    row_index = jnp.arange(rows_dev, dtype=jnp.int32)
    anchor = lax.axis_index("pb") * rows_dev + row_index
    positions = first + anchor
    max_pos = first + (lax.axis_index("pb") + 1) * rows_dev - 1
    attended = by_heads(queries, keys, values, positions, max_pos)
    partial = jnp.dot(attended, out_weight, preferred_element_type=jnp.float32)
    n_chip = lax.axis_size("kx")
    n_core = lax.axis_size("kc")
    partial = partial.reshape(n_chip, n_core, rows_dev // (n_chip * n_core), partial.shape[1])
    core = lax.axis_index("kc")
    mine = lax.dynamic_index_in_dim(partial, core, 1, keepdims=False)
    theirs = lax.dynamic_index_in_dim(partial, 1 - core, 1, keepdims=False)
    on_chip = mine + lax.ppermute(theirs, "kc", [(0, 1), (1, 0)])
    parts = lax.all_to_all(
        on_chip.astype(jnp.bfloat16), "kx", split_axis=0, concat_axis=0, tiled=True
    )
    return jnp.sum(parts.astype(jnp.float32), axis=0)


def solution(mesh):
    n_pb, n_kv = mesh.devices.shape
    split = Mesh(mesh.devices.reshape(n_pb, n_kv // 2, 2), ("pb", "kx", "kc"))
    in_specs = (P(), P("pb", KV), P(KV, None), P(KV, None), P(KV, None))
    out_specs = P(("pb",) + KV, None)
    return jax.shard_map(
        per_device, mesh=split, in_specs=in_specs, out_specs=out_specs, check_vma=False
    )
```

```python
import jax
import jax.numpy as jnp
from jax import lax
from jax.experimental import pallas as pl
from jax.experimental.pallas import tpu as pltpu
from jax.sharding import Mesh, PartitionSpec as P

HQ = 32
KVH = 16
HD = 128
CAP = 50
SCALAR = 144
KV = ("kx", "kc")
TQ = 256


def block_kernel(sc_ref, q_ref, k_ref, v_ref, m_ref, l_ref, acc_ref, m_out, l_out, acc_out):
    tq = q_ref.shape[0]
    tk = k_ref.shape[0]
    row_first = sc_ref[0] + (pl.program_id(0) * tq) % sc_ref[2]
    key_first = sc_ref[1]

    @pl.when(key_first > row_first + tq - 1)
    def _skip():
        m_out[...] = m_ref[...]
        l_out[...] = l_ref[...]
        acc_out[...] = acc_ref[...]

    @pl.when(key_first <= row_first + tq - 1)
    def _attend():
        raw = lax.dot_general(
            q_ref[...], k_ref[...], (((1,), (1,)), ((), ())), preferred_element_type=jnp.float32
        )
        scores = CAP * jnp.tanh(raw * (SCALAR ** (-0.5) / CAP))
        q_pos = row_first + lax.broadcasted_iota(jnp.int32, (tq, tk), 0)
        k_pos = key_first + lax.broadcasted_iota(jnp.int32, (tq, tk), 1)
        kept = k_pos <= q_pos
        scores = jnp.where(kept, scores, -1e30)
        top = m_ref[...]
        new_top = jnp.maximum(top, jnp.max(scores, axis=1, keepdims=True))
        keep = jnp.exp(top - new_top)
        prob = jnp.where(kept, jnp.exp(scores - new_top), 0.0)
        l_out[...] = l_ref[...] * keep + jnp.sum(prob, axis=1, keepdims=True)
        acc_out[...] = acc_ref[...] * keep + jnp.dot(
            prob.astype(jnp.bfloat16), v_ref[...], preferred_element_type=jnp.float32
        )
        m_out[...] = new_top


def attend_kernel(scalars, q, block, top, total, summed):
    n_q, hd = q.shape
    n_k = block.shape[1]
    tq = min(TQ, n_q)
    row = lambda i, sc: (i, 0)
    grid_spec = pltpu.PrefetchScalarGridSpec(
        num_scalar_prefetch=1,
        grid=(n_q // tq,),
        in_specs=[
            pl.BlockSpec((tq, hd), row),
            pl.BlockSpec((None, n_k, hd), lambda i, sc: (0, 0, 0)),
            pl.BlockSpec((None, n_k, hd), lambda i, sc: (1, 0, 0)),
            pl.BlockSpec((tq, 1), row),
            pl.BlockSpec((tq, 1), row),
            pl.BlockSpec((tq, hd), row),
        ],
        out_specs=[
            pl.BlockSpec((tq, 1), row),
            pl.BlockSpec((tq, 1), row),
            pl.BlockSpec((tq, hd), row),
        ],
    )
    return pl.pallas_call(
        block_kernel,
        grid_spec=grid_spec,
        out_shape=(
            jax.ShapeDtypeStruct(top.shape, jnp.float32),
            jax.ShapeDtypeStruct(total.shape, jnp.float32),
            jax.ShapeDtypeStruct(summed.shape, jnp.float32),
        ),
        input_output_aliases={4: 0, 5: 1, 6: 2},
    )(scalars, q, block, block, top, total, summed)


def by_heads(queries, keys, values, row_first):
    n_kv = lax.axis_size(KV)
    me = lax.axis_index(KV)
    group = HQ // KVH
    rows_dev = queries.shape[0]
    key_dev = keys.shape[0]
    kv_local = keys.shape[1] // (n_kv * HD)
    kv_feat = kv_local * HD
    n_q = kv_local * group * rows_dev
    q_block = queries.reshape(rows_dev, kv_local * group, HD).transpose(1, 0, 2).reshape(n_q, HD)
    top = jnp.full((n_q, 1), -1e30, jnp.float32)
    total = jnp.zeros((n_q, 1), jnp.float32)
    summed = jnp.zeros((n_q, HD), jnp.float32)
    for shift in range(n_kv):
        dest = (me + shift) % n_kv
        src = (me - shift) % n_kv
        block = jnp.stack(
            (
                lax.dynamic_slice_in_dim(keys, dest * kv_feat, kv_feat, 1),
                lax.dynamic_slice_in_dim(values, dest * kv_feat, kv_feat, 1),
            ),
            axis=0,
        )
        if shift:
            block = lax.ppermute(block, KV, [(j, (j + shift) % n_kv) for j in range(n_kv)])
        scalars = jnp.stack([row_first, src * key_dev, jnp.int32(rows_dev)]).astype(jnp.int32)
        top, total, summed = attend_kernel(scalars, q_block, block, top, total, summed)
    mixed = (summed / total).astype(jnp.bfloat16)
    return mixed.reshape(kv_local * group, rows_dev, HD).transpose(1, 0, 2).reshape(rows_dev, n_q // rows_dev * HD)


def per_device(slab_start, queries, keys, values, out_weight):
    rows_dev = queries.shape[0]
    row_first = slab_start[0] + lax.axis_index("pb") * rows_dev
    attended = by_heads(queries, keys, values, row_first)
    partial = jnp.dot(attended, out_weight, preferred_element_type=jnp.float32)
    n_chip = lax.axis_size("kx")
    n_core = lax.axis_size("kc")
    partial = partial.reshape(n_chip, n_core, rows_dev // (n_chip * n_core), partial.shape[1])
    core = lax.axis_index("kc")
    mine = lax.dynamic_index_in_dim(partial, core, 1, keepdims=False)
    theirs = lax.dynamic_index_in_dim(partial, 1 - core, 1, keepdims=False)
    on_chip = mine + lax.ppermute(theirs, "kc", [(0, 1), (1, 0)])
    parts = lax.all_to_all(
        on_chip.astype(jnp.bfloat16), "kx", split_axis=0, concat_axis=0, tiled=True
    )
    return jnp.sum(parts.astype(jnp.float32), axis=0)


def solution(mesh):
    n_pb, n_kv = mesh.devices.shape
    split = Mesh(mesh.devices.reshape(n_pb, n_kv // 2, 2), ("pb", "kx", "kc"))
    in_specs = (P(), P("pb", KV), P(KV, None), P(KV, None), P(KV, None))
    out_specs = P(("pb",) + KV, None)
    return jax.shard_map(
        per_device, mesh=split, in_specs=in_specs, out_specs=out_specs, check_vma=False
    )
```

```python
import jax
import jax.numpy as jnp
from jax import lax
from jax.experimental import pallas as pl
from jax.experimental.pallas import tpu as pltpu
from jax.sharding import Mesh, PartitionSpec as P

HQ = 32
KVH = 16
HD = 128
CAP = 50
SCALAR = 144
KV = ("kx", "kc")
TQ = 256


def block_kernel(sc_ref, q_ref, k_ref, v_ref, l_ref, acc_ref, l_out, acc_out):
    tq = q_ref.shape[0]
    tk = k_ref.shape[0]
    row_first = sc_ref[0] + (pl.program_id(0) * tq) % sc_ref[2]
    row_last = row_first + tq - 1
    key_first = sc_ref[1]
    key_last = key_first + tk - 1

    def update(masked):
        raw = lax.dot_general(
            q_ref[...], k_ref[...], (((1,), (1,)), ((), ())), preferred_element_type=jnp.float32
        )
        prob = jnp.exp(CAP * jnp.tanh(raw * (SCALAR ** (-0.5) / CAP)))
        if masked:
            q_pos = row_first + lax.broadcasted_iota(jnp.int32, (tq, tk), 0)
            k_pos = key_first + lax.broadcasted_iota(jnp.int32, (tq, tk), 1)
            prob = jnp.where(k_pos <= q_pos, prob, 0.0)
        l_out[...] = l_ref[...] + jnp.sum(prob, axis=1, keepdims=True)
        acc_out[...] = acc_ref[...] + jnp.dot(
            prob.astype(jnp.bfloat16), v_ref[...], preferred_element_type=jnp.float32
        )

    @pl.when(key_first > row_last)
    def _skip():
        l_out[...] = l_ref[...]
        acc_out[...] = acc_ref[...]

    @pl.when(key_last <= row_first)
    def _full():
        update(False)

    @pl.when(jnp.logical_and(key_first <= row_last, key_last > row_first))
    def _diagonal():
        update(True)


def attend_kernel(scalars, q, block, total, summed):
    n_q, hd = q.shape
    n_k = block.shape[1]
    tq = min(TQ, n_q)
    row = lambda i, sc: (i, 0)
    grid_spec = pltpu.PrefetchScalarGridSpec(
        num_scalar_prefetch=1,
        grid=(n_q // tq,),
        in_specs=[
            pl.BlockSpec((tq, hd), row),
            pl.BlockSpec((None, n_k, hd), lambda i, sc: (0, 0, 0)),
            pl.BlockSpec((None, n_k, hd), lambda i, sc: (1, 0, 0)),
            pl.BlockSpec((tq, 1), row),
            pl.BlockSpec((tq, hd), row),
        ],
        out_specs=[
            pl.BlockSpec((tq, 1), row),
            pl.BlockSpec((tq, hd), row),
        ],
    )
    return pl.pallas_call(
        block_kernel,
        grid_spec=grid_spec,
        out_shape=(
            jax.ShapeDtypeStruct(total.shape, jnp.float32),
            jax.ShapeDtypeStruct(summed.shape, jnp.float32),
        ),
        input_output_aliases={4: 0, 5: 1},
    )(scalars, q, block, block, total, summed)


def by_heads(queries, keys, values, row_first):
    n_kv = lax.axis_size(KV)
    me = lax.axis_index(KV)
    group = HQ // KVH
    rows_dev = queries.shape[0]
    key_dev = keys.shape[0]
    kv_local = keys.shape[1] // (n_kv * HD)
    kv_feat = kv_local * HD
    n_q = kv_local * group * rows_dev
    q_block = queries.reshape(rows_dev, kv_local * group, HD).transpose(1, 0, 2).reshape(n_q, HD)
    total = jnp.zeros((n_q, 1), jnp.float32)
    summed = jnp.zeros((n_q, HD), jnp.float32)
    for shift in range(n_kv):
        dest = (me + shift) % n_kv
        src = (me - shift) % n_kv
        block = jnp.stack(
            (
                lax.dynamic_slice_in_dim(keys, dest * kv_feat, kv_feat, 1),
                lax.dynamic_slice_in_dim(values, dest * kv_feat, kv_feat, 1),
            ),
            axis=0,
        )
        if shift:
            block = lax.ppermute(block, KV, [(j, (j + shift) % n_kv) for j in range(n_kv)])
        scalars = jnp.stack([row_first, src * key_dev, jnp.int32(rows_dev)]).astype(jnp.int32)
        total, summed = attend_kernel(scalars, q_block, block, total, summed)
    mixed = (summed / total).astype(jnp.bfloat16)
    return mixed.reshape(kv_local * group, rows_dev, HD).transpose(1, 0, 2).reshape(rows_dev, n_q // rows_dev * HD)


def per_device(slab_start, queries, keys, values, out_weight):
    rows_dev = queries.shape[0]
    row_first = slab_start[0] + lax.axis_index("pb") * rows_dev
    attended = by_heads(queries, keys, values, row_first)
    partial = jnp.dot(attended, out_weight, preferred_element_type=jnp.float32)
    n_chip = lax.axis_size("kx")
    n_core = lax.axis_size("kc")
    partial = partial.reshape(n_chip, n_core, rows_dev // (n_chip * n_core), partial.shape[1])
    core = lax.axis_index("kc")
    mine = lax.dynamic_index_in_dim(partial, core, 1, keepdims=False)
    theirs = lax.dynamic_index_in_dim(partial, 1 - core, 1, keepdims=False)
    on_chip = mine + lax.ppermute(theirs, "kc", [(0, 1), (1, 0)])
    parts = lax.all_to_all(
        on_chip.astype(jnp.bfloat16), "kx", split_axis=0, concat_axis=0, tiled=True
    )
    return jnp.sum(parts.astype(jnp.float32), axis=0)


def solution(mesh):
    n_pb, n_kv = mesh.devices.shape
    split = Mesh(mesh.devices.reshape(n_pb, n_kv // 2, 2), ("pb", "kx", "kc"))
    in_specs = (P(), P("pb", KV), P(KV, None), P(KV, None), P(KV, None))
    out_specs = P(("pb",) + KV, None)
    return jax.shard_map(
        per_device, mesh=split, in_specs=in_specs, out_specs=out_specs, check_vma=False
    )
```

```python
import jax
import jax.numpy as jnp
from jax import lax
from jax.experimental import pallas as pl
from jax.experimental.pallas import tpu as pltpu
from jax.sharding import Mesh, PartitionSpec as P

HQ = 32
KVH = 16
HD = 128
CAP = 50
SCALAR = 144
KV = ("kx", "kc")
TQ = 256


def block_kernel(sc_ref, q_ref, k_ref, v_ref, l_ref, acc_ref, l_out, acc_out):
    tq = q_ref.shape[0]
    tk = k_ref.shape[0]
    row_first = sc_ref[0] + (pl.program_id(0) * tq) % sc_ref[2]
    row_last = row_first + tq - 1
    key_first = sc_ref[1]
    key_last = key_first + tk - 1

    def update(masked):
        raw = lax.dot_general(
            q_ref[...], k_ref[...], (((1,), (1,)), ((), ())), preferred_element_type=jnp.float32
        )
        prob = jnp.exp(CAP * jnp.tanh(raw * (SCALAR ** (-0.5) / CAP)))
        if masked:
            q_pos = row_first + lax.broadcasted_iota(jnp.int32, (tq, tk), 0)
            k_pos = key_first + lax.broadcasted_iota(jnp.int32, (tq, tk), 1)
            prob = jnp.where(k_pos <= q_pos, prob, 0.0)
        l_out[...] = l_ref[...] + jnp.sum(prob, axis=1, keepdims=True)
        acc_out[...] = acc_ref[...] + jnp.dot(
            prob.astype(jnp.bfloat16), v_ref[...], preferred_element_type=jnp.float32
        )

    @pl.when(key_first > row_last)
    def _skip():
        l_out[...] = l_ref[...]
        acc_out[...] = acc_ref[...]

    @pl.when(key_last <= row_first)
    def _full():
        update(False)

    @pl.when(jnp.logical_and(key_first <= row_last, key_last > row_first))
    def _diagonal():
        update(True)


def attend_kernel(scalars, q, block, total, summed):
    n_q, hd = q.shape
    n_k = block.shape[1]
    tq = min(TQ, n_q)
    row = lambda i, sc: (i, 0)
    grid_spec = pltpu.PrefetchScalarGridSpec(
        num_scalar_prefetch=1,
        grid=(n_q // tq,),
        in_specs=[
            pl.BlockSpec((tq, hd), row),
            pl.BlockSpec((None, n_k, hd), lambda i, sc: (0, 0, 0)),
            pl.BlockSpec((None, n_k, hd), lambda i, sc: (1, 0, 0)),
            pl.BlockSpec((tq, 1), row),
            pl.BlockSpec((tq, hd), row),
        ],
        out_specs=[
            pl.BlockSpec((tq, 1), row),
            pl.BlockSpec((tq, hd), row),
        ],
    )
    return pl.pallas_call(
        block_kernel,
        grid_spec=grid_spec,
        out_shape=(
            jax.ShapeDtypeStruct(total.shape, jnp.float32),
            jax.ShapeDtypeStruct(summed.shape, jnp.float32),
        ),
        input_output_aliases={4: 0, 5: 1},
        cost_estimate=pl.CostEstimate(
            flops=4 * n_q * n_k * hd,
            transcendentals=2 * n_q * n_k,
            bytes_accessed=2 * (n_q + 2 * n_k) * hd + 8 * n_q * (hd + 1),
        ),
    )(scalars, q, block, block, total, summed)


def by_heads(queries, keys, values, row_first):
    n_kv = lax.axis_size(KV)
    me = lax.axis_index(KV)
    group = HQ // KVH
    rows_dev = queries.shape[0]
    key_dev = keys.shape[0]
    kv_local = keys.shape[1] // (n_kv * HD)
    kv_feat = kv_local * HD
    n_q = kv_local * group * rows_dev
    q_block = queries.reshape(rows_dev, kv_local * group, HD).transpose(1, 0, 2).reshape(n_q, HD)
    total = jnp.zeros((n_q, 1), jnp.float32)
    summed = jnp.zeros((n_q, HD), jnp.float32)
    for shift in range(n_kv):
        dest = (me + shift) % n_kv
        src = (me - shift) % n_kv
        block = jnp.stack(
            (
                lax.dynamic_slice_in_dim(keys, dest * kv_feat, kv_feat, 1),
                lax.dynamic_slice_in_dim(values, dest * kv_feat, kv_feat, 1),
            ),
            axis=0,
        )
        if shift:
            block = lax.ppermute(block, KV, [(j, (j + shift) % n_kv) for j in range(n_kv)])
        scalars = jnp.stack([row_first, src * key_dev, jnp.int32(rows_dev)]).astype(jnp.int32)
        total, summed = attend_kernel(scalars, q_block, block, total, summed)
    mixed = (summed / total).astype(jnp.bfloat16)
    return mixed.reshape(kv_local * group, rows_dev, HD).transpose(1, 0, 2).reshape(rows_dev, n_q // rows_dev * HD)


def per_device(slab_start, queries, keys, values, out_weight):
    rows_dev = queries.shape[0]
    row_first = slab_start[0] + lax.axis_index("pb") * rows_dev
    attended = by_heads(queries, keys, values, row_first)
    partial = jnp.dot(attended, out_weight, preferred_element_type=jnp.float32)
    n_chip = lax.axis_size("kx")
    n_core = lax.axis_size("kc")
    partial = partial.reshape(n_chip, n_core, rows_dev // (n_chip * n_core), partial.shape[1])
    core = lax.axis_index("kc")
    mine = lax.dynamic_index_in_dim(partial, core, 1, keepdims=False)
    theirs = lax.dynamic_index_in_dim(partial, 1 - core, 1, keepdims=False)
    on_chip = mine + lax.ppermute(theirs, "kc", [(0, 1), (1, 0)])
    parts = lax.all_to_all(
        on_chip.astype(jnp.bfloat16), "kx", split_axis=0, concat_axis=0, tiled=True
    )
    return jnp.sum(parts.astype(jnp.float32), axis=0)


def solution(mesh):
    n_pb, n_kv = mesh.devices.shape
    split = Mesh(mesh.devices.reshape(n_pb, n_kv // 2, 2), ("pb", "kx", "kc"))
    in_specs = (P(), P("pb", KV), P(KV, None), P(KV, None), P(KV, None))
    out_specs = P(("pb",) + KV, None)
    return jax.shard_map(
        per_device, mesh=split, in_specs=in_specs, out_specs=out_specs, check_vma=False
    )
```

```python
import jax
import jax.numpy as jnp
from jax import lax
from jax.experimental import pallas as pl
from jax.experimental.pallas import tpu as pltpu
from jax.sharding import Mesh, PartitionSpec as P

HQ = 32
KVH = 16
HD = 128
CAP = 50
SCALAR = 144
KV = ("kx", "kc")
TQ = 256


def block_kernel(sc_ref, q_ref, k_ref, v_ref, l_ref, acc_ref, l_out, acc_out):
    tq = q_ref.shape[0]
    tk = k_ref.shape[0]
    row_first = sc_ref[0] + (pl.program_id(0) * tq) % sc_ref[2]
    row_last = row_first + tq - 1
    key_first = sc_ref[1]
    key_last = key_first + tk - 1

    def update(masked):
        raw = lax.dot_general(
            q_ref[...], k_ref[...], (((1,), (1,)), ((), ())), preferred_element_type=jnp.float32
        )
        prob = jnp.exp(CAP * jnp.tanh(raw * (SCALAR ** (-0.5) / CAP)))
        if masked:
            q_pos = row_first + lax.broadcasted_iota(jnp.int32, (tq, tk), 0)
            k_pos = key_first + lax.broadcasted_iota(jnp.int32, (tq, tk), 1)
            prob = jnp.where(k_pos <= q_pos, prob, 0.0)
        l_out[...] = l_ref[...] + jnp.sum(prob, axis=1, keepdims=True)
        acc_out[...] = acc_ref[...] + jnp.dot(
            prob.astype(jnp.bfloat16), v_ref[...], preferred_element_type=jnp.float32
        )

    @pl.when(key_first > row_last)
    def _skip():
        l_out[...] = l_ref[...]
        acc_out[...] = acc_ref[...]

    @pl.when(key_last <= row_first)
    def _full():
        update(False)

    @pl.when(jnp.logical_and(key_first <= row_last, key_last > row_first))
    def _diagonal():
        update(True)


def attend_kernel(scalars, q, block, total, summed):
    n_q, hd = q.shape
    n_k = block.shape[1]
    tq = min(TQ, n_q)
    row = lambda i, sc: (i, 0)
    grid_spec = pltpu.PrefetchScalarGridSpec(
        num_scalar_prefetch=1,
        grid=(n_q // tq,),
        in_specs=[
            pl.BlockSpec((tq, hd), row),
            pl.BlockSpec((None, n_k, hd), lambda i, sc: (0, 0, 0)),
            pl.BlockSpec((None, n_k, hd), lambda i, sc: (1, 0, 0)),
            pl.BlockSpec((tq, 1), row),
            pl.BlockSpec((tq, hd), row),
        ],
        out_specs=[
            pl.BlockSpec((tq, 1), row),
            pl.BlockSpec((tq, hd), row),
        ],
    )
    return pl.pallas_call(
        block_kernel,
        grid_spec=grid_spec,
        out_shape=(
            jax.ShapeDtypeStruct(total.shape, jnp.float32),
            jax.ShapeDtypeStruct(summed.shape, jnp.float32),
        ),
        input_output_aliases={4: 0, 5: 1},
        cost_estimate=pl.CostEstimate(
            flops=4 * n_q * n_k * hd,
            transcendentals=2 * n_q * n_k,
            bytes_accessed=2 * (n_q + 2 * n_k) * hd + 8 * n_q * (hd + 1),
        ),
    )(scalars, q, block, block, total, summed)


def by_heads(queries, keys, values, row_first):
    n_kv = lax.axis_size(KV)
    me = lax.axis_index(KV)
    group = HQ // KVH
    rows_dev = queries.shape[0]
    key_dev = keys.shape[0]
    kv_local = keys.shape[1] // (n_kv * HD)
    kv_feat = kv_local * HD
    n_q = kv_local * group * rows_dev
    q_block = queries.reshape(rows_dev, kv_local * group, HD).transpose(1, 0, 2).reshape(n_q, HD)
    total = jnp.zeros((n_q, 1), jnp.float32)
    summed = jnp.zeros((n_q, HD), jnp.float32)
    for shift in range(n_kv):
        dest = (me + shift) % n_kv
        src = (me - shift) % n_kv
        block = jnp.stack(
            (
                lax.dynamic_slice_in_dim(keys, dest * kv_feat, kv_feat, 1),
                lax.dynamic_slice_in_dim(values, dest * kv_feat, kv_feat, 1),
            ),
            axis=0,
        )
        if shift:
            block = lax.ppermute(block, KV, [(j, (j + shift) % n_kv) for j in range(n_kv)])
        scalars = jnp.stack([row_first, src * key_dev, jnp.int32(rows_dev)]).astype(jnp.int32)
        total, summed = attend_kernel(scalars, q_block, block, total, summed)
    mixed = (summed / total).astype(jnp.bfloat16)
    return mixed.reshape(kv_local * group, rows_dev, HD).transpose(1, 0, 2).reshape(rows_dev, n_q // rows_dev * HD)


def per_device(slab_start, queries, keys, values, out_weight):
    rows_dev = queries.shape[0]
    row_first = slab_start[0] + lax.axis_index("pb") * rows_dev
    attended = by_heads(queries, keys, values, row_first)
    partial = jnp.dot(attended, out_weight, preferred_element_type=jnp.float32)
    n_chip = lax.axis_size("kx")
    n_core = lax.axis_size("kc")
    partial = partial.reshape(n_chip, n_core, rows_dev // (n_chip * n_core), partial.shape[1])
    core = lax.axis_index("kc")
    mine = lax.dynamic_index_in_dim(partial, core, 1, keepdims=False)
    theirs = lax.dynamic_index_in_dim(partial, 1 - core, 1, keepdims=False).astype(jnp.bfloat16)
    on_chip = mine + lax.ppermute(theirs, "kc", [(0, 1), (1, 0)]).astype(jnp.float32)
    chip = lax.axis_index("kx")
    result = lax.dynamic_index_in_dim(on_chip, chip, 0, keepdims=False)
    for shift in range(1, n_chip):
        part = lax.dynamic_index_in_dim(on_chip, (chip + shift) % n_chip, 0, keepdims=False)
        moved = lax.ppermute(
            part.astype(jnp.bfloat16), "kx", [(k, (k + shift) % n_chip) for k in range(n_chip)]
        )
        result = result + moved.astype(jnp.float32)
    return result


def solution(mesh):
    n_pb, n_kv = mesh.devices.shape
    split = Mesh(mesh.devices.reshape(n_pb, n_kv // 2, 2), ("pb", "kx", "kc"))
    in_specs = (P(), P("pb", KV), P(KV, None), P(KV, None), P(KV, None))
    out_specs = P(("pb",) + KV, None)
    return jax.shard_map(
        per_device, mesh=split, in_specs=in_specs, out_specs=out_specs, check_vma=False
    )
```

```python
import functools

import jax
import jax.numpy as jnp
from jax import lax
from jax.experimental import pallas as pl
from jax.experimental.pallas import tpu as pltpu
from jax.sharding import Mesh, PartitionSpec as P

HQ = 32
KVH = 16
HD = 128
CAP = 50
SCALAR = 144
KV = ("kx", "kc")
HALVES = 2


def block_kernel(sc_ref, q_ref, k_ref, v_ref, l_ref, acc_ref, l_out, acc_out, *, run, stride):
    tq = q_ref.shape[0]
    tk = k_ref.shape[0]
    row_first = sc_ref[0]
    row_last = row_first + (tq // run - 1) * stride + run - 1
    key_first = sc_ref[1]
    key_last = key_first + tk - 1

    def update(masked):
        raw = lax.dot_general(
            q_ref[...], k_ref[...], (((1,), (1,)), ((), ())), preferred_element_type=jnp.float32
        )
        prob = jnp.exp(CAP * jnp.tanh(raw * (SCALAR ** (-0.5) / CAP)))
        if masked:
            rows = lax.broadcasted_iota(jnp.int32, (tq, tk), 0)
            shift = run.bit_length() - 1
            q_pos = row_first + lax.shift_right_logical(rows, shift) * stride + (rows & (run - 1))
            k_pos = key_first + lax.broadcasted_iota(jnp.int32, (tq, tk), 1)
            prob = jnp.where(k_pos <= q_pos, prob, 0.0)
        l_out[...] = l_ref[...] + jnp.sum(prob, axis=1, keepdims=True)
        acc_out[...] = acc_ref[...] + jnp.dot(
            prob.astype(jnp.bfloat16), v_ref[...], preferred_element_type=jnp.float32
        )

    @pl.when(key_first > row_last)
    def _skip():
        l_out[...] = l_ref[...]
        acc_out[...] = acc_ref[...]

    @pl.when(key_last <= row_first)
    def _full():
        update(False)

    @pl.when(jnp.logical_and(key_first <= row_last, key_last > row_first))
    def _diagonal():
        update(True)


def attend_kernel(scalars, q, block, total, summed, run, stride, tq):
    n_q, hd = q.shape
    n_k = block.shape[1]
    row = lambda i, sc: (i, 0)
    grid_spec = pltpu.PrefetchScalarGridSpec(
        num_scalar_prefetch=1,
        grid=(n_q // tq,),
        in_specs=[
            pl.BlockSpec((tq, hd), row),
            pl.BlockSpec((None, n_k, hd), lambda i, sc: (0, 0, 0)),
            pl.BlockSpec((None, n_k, hd), lambda i, sc: (1, 0, 0)),
            pl.BlockSpec((tq, 1), row),
            pl.BlockSpec((tq, hd), row),
        ],
        out_specs=[
            pl.BlockSpec((tq, 1), row),
            pl.BlockSpec((tq, hd), row),
        ],
    )
    return pl.pallas_call(
        functools.partial(block_kernel, run=run, stride=stride),
        grid_spec=grid_spec,
        out_shape=(
            jax.ShapeDtypeStruct(total.shape, jnp.float32),
            jax.ShapeDtypeStruct(summed.shape, jnp.float32),
        ),
        input_output_aliases={4: 0, 5: 1},
        cost_estimate=pl.CostEstimate(
            flops=4 * n_q * n_k * hd,
            transcendentals=2 * n_q * n_k,
            bytes_accessed=2 * (n_q + 2 * n_k) * hd + 8 * n_q * (hd + 1),
        ),
    )(scalars, q, block, block, total, summed)


def reduce_pieces(partial):
    n_chip = lax.axis_size("kx")
    n_core = lax.axis_size("kc")
    partial = partial.reshape(n_chip, n_core, -1, partial.shape[1])
    core = lax.axis_index("kc")
    mine = lax.dynamic_index_in_dim(partial, core, 1, keepdims=False)
    theirs = lax.dynamic_index_in_dim(partial, 1 - core, 1, keepdims=False).astype(jnp.bfloat16)
    on_chip = mine + lax.ppermute(theirs, "kc", [(0, 1), (1, 0)]).astype(jnp.float32)
    chip = lax.axis_index("kx")
    pieces = [lax.dynamic_index_in_dim(on_chip, chip, 0, keepdims=False)]
    for shift in range(1, n_chip):
        part = lax.dynamic_index_in_dim(on_chip, (chip + shift) % n_chip, 0, keepdims=False)
        pieces.append(
            lax.ppermute(
                part.astype(jnp.bfloat16), "kx", [(k, (k + shift) % n_chip) for k in range(n_chip)]
            )
        )
    return pieces


def add_pieces(pieces):
    result = pieces[0]
    for piece in pieces[1:]:
        result = result + piece.astype(jnp.float32)
    return result


def per_device(slab_start, queries, keys, values, out_weight):
    n_kv = lax.axis_size(KV)
    me = lax.axis_index(KV)
    group = HQ // KVH
    rows_dev = queries.shape[0]
    row_first = slab_start[0] + lax.axis_index("pb") * rows_dev
    key_dev = keys.shape[0]
    kv_local = keys.shape[1] // (n_kv * HD)
    kv_feat = kv_local * HD
    heads = kv_local * group
    chunk = rows_dev // n_kv
    run = chunk // HALVES
    q_halves = (
        queries.reshape(n_kv, HALVES, run, heads, HD)
        .transpose(1, 3, 0, 2, 4)
        .reshape(HALVES, heads * n_kv * run, HD)
    )
    n_q = heads * n_kv * run
    tq = n_kv * run
    state = [
        (jnp.zeros((n_q, 1), jnp.float32), jnp.zeros((n_q, HD), jnp.float32))
        for _ in range(HALVES)
    ]
    blocks = []
    for shift in range(n_kv):
        dest = (me + shift) % n_kv
        src = (me - shift) % n_kv
        block = jnp.stack(
            (
                lax.dynamic_slice_in_dim(keys, dest * kv_feat, kv_feat, 1),
                lax.dynamic_slice_in_dim(values, dest * kv_feat, kv_feat, 1),
            ),
            axis=0,
        )
        if shift:
            block = lax.ppermute(block, KV, [(j, (j + shift) % n_kv) for j in range(n_kv)])
        blocks.append((block, src))
    results = []
    pending = []
    late = n_kv // 2 - 2
    for half in range(HALVES):
        for index, (block, src) in enumerate(blocks):
            at = index - late
            if 0 <= at < len(pending):
                pending[at], state[half] = lax.optimization_barrier((pending[at], state[half]))
            scalars = jnp.stack([row_first + half * run, src * key_dev]).astype(jnp.int32)
            state[half] = attend_kernel(
                scalars, q_halves[half], block, *state[half], run, chunk, tq
            )
        if pending:
            results.append(add_pieces(pending))
        total, summed = state[half]
        mixed = (summed / total).astype(jnp.bfloat16)
        attended = (
            mixed.reshape(heads, n_kv * run, HD).transpose(1, 0, 2).reshape(n_kv * run, heads * HD)
        )
        partial = jnp.dot(attended, out_weight, preferred_element_type=jnp.float32)
        pending = reduce_pieces(partial)
    results.append(add_pieces(pending))
    return jnp.concatenate(results, axis=0)


def solution(mesh):
    n_pb, n_kv = mesh.devices.shape
    split = Mesh(mesh.devices.reshape(n_pb, n_kv // 2, 2), ("pb", "kx", "kc"))
    in_specs = (P(), P("pb", KV), P(KV, None), P(KV, None), P(KV, None))
    out_specs = P(("pb",) + KV, None)
    return jax.shard_map(
        per_device, mesh=split, in_specs=in_specs, out_specs=out_specs, check_vma=False
    )
```

```python
import jax
import jax.numpy as jnp
from jax import lax
from jax.experimental import pallas as pl
from jax.experimental.pallas import tpu as pltpu
from jax.sharding import Mesh, PartitionSpec as P

HQ = 32
KVH = 16
HD = 128
CAP = 50
SCALAR = 144
KV = ("kx", "kc")
TQ = 256


def block_kernel(sc_ref, q_ref, k_ref, v_ref, l_ref, acc_ref, l_out, acc_out):
    tq = q_ref.shape[0]
    tk = k_ref.shape[0]
    row_first = sc_ref[0] + (pl.program_id(0) * tq) % sc_ref[2]
    row_last = row_first + tq - 1
    key_first = sc_ref[1]
    key_last = key_first + tk - 1

    def update(masked):
        raw = lax.dot_general(
            q_ref[...], k_ref[...], (((1,), (1,)), ((), ())), preferred_element_type=jnp.float32
        )
        prob = jnp.exp(CAP * jnp.tanh(raw * (SCALAR ** (-0.5) / CAP)))
        if masked:
            q_pos = row_first + lax.broadcasted_iota(jnp.int32, (tq, tk), 0)
            k_pos = key_first + lax.broadcasted_iota(jnp.int32, (tq, tk), 1)
            prob = jnp.where(k_pos <= q_pos, prob, 0.0)
        l_out[...] = l_ref[...] + jnp.sum(prob, axis=1, keepdims=True)
        acc_out[...] = acc_ref[...] + jnp.dot(
            prob.astype(jnp.bfloat16), v_ref[...], preferred_element_type=jnp.float32
        )

    @pl.when(key_first > row_last)
    def _skip():
        l_out[...] = l_ref[...]
        acc_out[...] = acc_ref[...]

    @pl.when(key_last <= row_first)
    def _full():
        update(False)

    @pl.when(jnp.logical_and(key_first <= row_last, key_last > row_first))
    def _diagonal():
        update(True)


def attend_kernel(scalars, q, block, index, total, summed):
    n_q, hd = q.shape
    n_k = block.shape[2]
    tq = min(TQ, n_q)
    row = lambda i, sc: (i, 0)
    grid_spec = pltpu.PrefetchScalarGridSpec(
        num_scalar_prefetch=1,
        grid=(n_q // tq,),
        in_specs=[
            pl.BlockSpec((tq, hd), row),
            pl.BlockSpec((None, None, n_k, hd), lambda i, sc: (0, index, 0, 0)),
            pl.BlockSpec((None, None, n_k, hd), lambda i, sc: (1, index, 0, 0)),
            pl.BlockSpec((tq, 1), row),
            pl.BlockSpec((tq, hd), row),
        ],
        out_specs=[
            pl.BlockSpec((tq, 1), row),
            pl.BlockSpec((tq, hd), row),
        ],
    )
    return pl.pallas_call(
        block_kernel,
        grid_spec=grid_spec,
        out_shape=(
            jax.ShapeDtypeStruct(total.shape, jnp.float32),
            jax.ShapeDtypeStruct(summed.shape, jnp.float32),
        ),
        input_output_aliases={4: 0, 5: 1},
        cost_estimate=pl.CostEstimate(
            flops=4 * n_q * n_k * hd,
            transcendentals=2 * n_q * n_k,
            bytes_accessed=2 * (n_q + 2 * n_k) * hd + 8 * n_q * (hd + 1),
        ),
    )(scalars, q, block, block, total, summed)


def by_heads(queries, keys, values, row_first):
    n_chip = lax.axis_size("kx")
    n_core = lax.axis_size("kc")
    chip = lax.axis_index("kx")
    core = lax.axis_index("kc")
    group = HQ // KVH
    rows_dev = queries.shape[0]
    key_dev = keys.shape[0]
    n_q = group * rows_dev
    q_block = queries.reshape(rows_dev, group, HD).transpose(1, 0, 2).reshape(n_q, HD)
    total = jnp.zeros((n_q, 1), jnp.float32)
    summed = jnp.zeros((n_q, HD), jnp.float32)
    per_core = (keys.reshape(key_dev, n_chip, n_core, HD), values.reshape(key_dev, n_chip, n_core, HD))

    def heads_of(which):
        return jnp.stack(
            [lax.dynamic_index_in_dim(part, which, 2, keepdims=False) for part in per_core]
        ).transpose(0, 2, 1, 3)

    own = heads_of(core)
    other = lax.ppermute(heads_of(1 - core), "kc", [(0, 1), (1, 0)])
    own_first = (chip * n_core + core) * key_dev
    other_first = (chip * n_core + 1 - core) * key_dev
    arrived = [
        (lax.dynamic_slice_in_dim(own, chip, 1, 1), own_first),
        (lax.dynamic_slice_in_dim(other, chip, 1, 1), other_first),
    ]
    for shift in range(1, n_chip):
        dest = (chip + shift) % n_chip
        src = (chip - shift) % n_chip
        payload = jnp.concatenate(
            [lax.dynamic_slice_in_dim(own, dest, 1, 1), lax.dynamic_slice_in_dim(other, dest, 1, 1)],
            axis=1,
        )
        moved = lax.ppermute(payload, "kx", [(k, (k + shift) % n_chip) for k in range(n_chip)])
        arrived.append((moved, (src * n_core + core) * key_dev))
        arrived.append((moved, (src * n_core + 1 - core) * key_dev))
    for number, (block, key_first) in enumerate(arrived):
        index = 0 if number < 2 else number % 2
        scalars = jnp.stack([row_first, key_first, jnp.int32(rows_dev)]).astype(jnp.int32)
        total, summed = attend_kernel(scalars, q_block, block, index, total, summed)
    mixed = (summed / total).astype(jnp.bfloat16)
    return mixed.reshape(group, rows_dev, HD).transpose(1, 0, 2).reshape(rows_dev, group * HD)


def per_device(slab_start, queries, keys, values, out_weight):
    rows_dev = queries.shape[0]
    row_first = slab_start[0] + lax.axis_index("pb") * rows_dev
    attended = by_heads(queries, keys, values, row_first)
    partial = jnp.dot(attended, out_weight, preferred_element_type=jnp.float32)
    n_chip = lax.axis_size("kx")
    n_core = lax.axis_size("kc")
    partial = partial.reshape(n_chip, n_core, rows_dev // (n_chip * n_core), partial.shape[1])
    core = lax.axis_index("kc")
    mine = lax.dynamic_index_in_dim(partial, core, 1, keepdims=False)
    theirs = lax.dynamic_index_in_dim(partial, 1 - core, 1, keepdims=False)
    on_chip = mine + lax.ppermute(theirs, "kc", [(0, 1), (1, 0)])
    parts = lax.all_to_all(
        on_chip.astype(jnp.bfloat16), "kx", split_axis=0, concat_axis=0, tiled=True
    )
    return jnp.sum(parts.astype(jnp.float32), axis=0)


def solution(mesh):
    n_pb, n_kv = mesh.devices.shape
    split = Mesh(mesh.devices.reshape(n_pb, n_kv // 2, 2), ("pb", "kx", "kc"))
    in_specs = (P(), P("pb", KV), P(KV, None), P(KV, None), P(KV, None))
    out_specs = P(("pb",) + KV, None)
    return jax.shard_map(
        per_device, mesh=split, in_specs=in_specs, out_specs=out_specs, check_vma=False
    )
```

```python
import jax
import jax.numpy as jnp
from jax import lax
from jax.experimental import pallas as pl
from jax.experimental.pallas import tpu as pltpu
from jax.sharding import Mesh, PartitionSpec as P

HQ = 32
KVH = 16
HD = 128
CAP = 50
SCALAR = 144
KV = ("kx", "kc")
TQ = 512


def block_kernel(sc_ref, q_ref, k_ref, v_ref, l_ref, acc_ref, l_out, acc_out):
    tq = q_ref.shape[0]
    tk = k_ref.shape[0]
    row_first = sc_ref[0] + (pl.program_id(0) * tq) % sc_ref[2]
    row_last = row_first + tq - 1
    key_first = sc_ref[1]
    key_last = key_first + tk - 1

    def update(masked):
        raw = lax.dot_general(
            q_ref[...], k_ref[...], (((1,), (1,)), ((), ())), preferred_element_type=jnp.float32
        )
        prob = jnp.exp(CAP * jnp.tanh(raw * (SCALAR ** (-0.5) / CAP)))
        if masked:
            q_pos = row_first + lax.broadcasted_iota(jnp.int32, (tq, tk), 0)
            k_pos = key_first + lax.broadcasted_iota(jnp.int32, (tq, tk), 1)
            prob = jnp.where(k_pos <= q_pos, prob, 0.0)
        l_out[...] = l_ref[...] + jnp.sum(prob, axis=1, keepdims=True)
        acc_out[...] = acc_ref[...] + jnp.dot(
            prob.astype(jnp.bfloat16), v_ref[...], preferred_element_type=jnp.float32
        )

    @pl.when(key_first > row_last)
    def _skip():
        l_out[...] = l_ref[...]
        acc_out[...] = acc_ref[...]

    @pl.when(key_last <= row_first)
    def _full():
        update(False)

    @pl.when(jnp.logical_and(key_first <= row_last, key_last > row_first))
    def _diagonal():
        update(True)


def attend_kernel(scalars, q, block, total, summed):
    n_q, hd = q.shape
    n_k = block.shape[1]
    tq = min(TQ, n_q)
    row = lambda i, sc: (i, 0)
    grid_spec = pltpu.PrefetchScalarGridSpec(
        num_scalar_prefetch=1,
        grid=(n_q // tq,),
        in_specs=[
            pl.BlockSpec((tq, hd), row),
            pl.BlockSpec((None, n_k, hd), lambda i, sc: (0, 0, 0)),
            pl.BlockSpec((None, n_k, hd), lambda i, sc: (1, 0, 0)),
            pl.BlockSpec((tq, 1), row),
            pl.BlockSpec((tq, hd), row),
        ],
        out_specs=[
            pl.BlockSpec((tq, 1), row),
            pl.BlockSpec((tq, hd), row),
        ],
    )
    return pl.pallas_call(
        block_kernel,
        grid_spec=grid_spec,
        out_shape=(
            jax.ShapeDtypeStruct(total.shape, jnp.float32),
            jax.ShapeDtypeStruct(summed.shape, jnp.float32),
        ),
        input_output_aliases={4: 0, 5: 1},
        cost_estimate=pl.CostEstimate(
            flops=4 * n_q * n_k * hd,
            transcendentals=2 * n_q * n_k,
            bytes_accessed=2 * (n_q + 2 * n_k) * hd + 8 * n_q * (hd + 1),
        ),
    )(scalars, q, block, block, total, summed)


def by_heads(queries, keys, values, row_first):
    n_kv = lax.axis_size(KV)
    me = lax.axis_index(KV)
    group = HQ // KVH
    rows_dev = queries.shape[0]
    key_dev = keys.shape[0]
    kv_local = keys.shape[1] // (n_kv * HD)
    kv_feat = kv_local * HD
    n_q = kv_local * group * rows_dev
    q_block = queries.reshape(rows_dev, kv_local * group, HD).transpose(1, 0, 2).reshape(n_q, HD)
    total = jnp.zeros((n_q, 1), jnp.float32)
    summed = jnp.zeros((n_q, HD), jnp.float32)
    for shift in range(n_kv):
        dest = (me + shift) % n_kv
        src = (me - shift) % n_kv
        block = jnp.stack(
            (
                lax.dynamic_slice_in_dim(keys, dest * kv_feat, kv_feat, 1),
                lax.dynamic_slice_in_dim(values, dest * kv_feat, kv_feat, 1),
            ),
            axis=0,
        )
        if shift:
            block = lax.ppermute(block, KV, [(j, (j + shift) % n_kv) for j in range(n_kv)])
        scalars = jnp.stack([row_first, src * key_dev, jnp.int32(rows_dev)]).astype(jnp.int32)
        total, summed = attend_kernel(scalars, q_block, block, total, summed)
    mixed = (summed / total).astype(jnp.bfloat16)
    return mixed.reshape(kv_local * group, rows_dev, HD).transpose(1, 0, 2).reshape(rows_dev, n_q // rows_dev * HD)


def per_device(slab_start, queries, keys, values, out_weight):
    rows_dev = queries.shape[0]
    row_first = slab_start[0] + lax.axis_index("pb") * rows_dev
    attended = by_heads(queries, keys, values, row_first)
    partial = jnp.dot(attended, out_weight, preferred_element_type=jnp.float32)
    n_chip = lax.axis_size("kx")
    n_core = lax.axis_size("kc")
    partial = partial.reshape(n_chip, n_core, rows_dev // (n_chip * n_core), partial.shape[1])
    core = lax.axis_index("kc")
    mine = lax.dynamic_index_in_dim(partial, core, 1, keepdims=False)
    theirs = lax.dynamic_index_in_dim(partial, 1 - core, 1, keepdims=False)
    on_chip = mine + lax.ppermute(theirs, "kc", [(0, 1), (1, 0)])
    parts = lax.all_to_all(
        on_chip.astype(jnp.bfloat16), "kx", split_axis=0, concat_axis=0, tiled=True
    )
    return jnp.sum(parts.astype(jnp.float32), axis=0)


def solution(mesh):
    n_pb, n_kv = mesh.devices.shape
    split = Mesh(mesh.devices.reshape(n_pb, n_kv // 2, 2), ("pb", "kx", "kc"))
    in_specs = (P(), P("pb", KV), P(KV, None), P(KV, None), P(KV, None))
    out_specs = P(("pb",) + KV, None)
    return jax.shard_map(
        per_device, mesh=split, in_specs=in_specs, out_specs=out_specs, check_vma=False
    )
```

```python
import jax
import jax.numpy as jnp
from jax import lax
from jax.experimental import pallas as pl
from jax.experimental.pallas import tpu as pltpu
from jax.sharding import Mesh, PartitionSpec as P

HQ = 32
KVH = 16
HD = 128
CAP = 50
SCALAR = 144
KV = ("kx", "kc")
TQ = 256


def block_kernel(sc_ref, q_ref, k_ref, v_ref, l_ref, acc_ref, l_out, acc_out):
    tq = q_ref.shape[0]
    tk = k_ref.shape[0]
    row_first = sc_ref[0] + (pl.program_id(0) * tq) % sc_ref[2]
    row_last = row_first + tq - 1
    key_first = sc_ref[1]
    key_last = key_first + tk - 1

    def update(masked):
        raw = lax.dot_general(
            q_ref[...], k_ref[...], (((1,), (1,)), ((), ())), preferred_element_type=jnp.float32
        )
        prob = jnp.exp(CAP * jnp.tanh(raw * (SCALAR ** (-0.5) / CAP)))
        if masked:
            q_pos = row_first + lax.broadcasted_iota(jnp.int32, (tq, tk), 0)
            k_pos = key_first + lax.broadcasted_iota(jnp.int32, (tq, tk), 1)
            prob = jnp.where(k_pos <= q_pos, prob, 0.0)
        l_out[...] = l_ref[...] + jnp.sum(prob, axis=1, keepdims=True)
        acc_out[...] = acc_ref[...] + jnp.dot(
            prob.astype(jnp.bfloat16), v_ref[...], preferred_element_type=jnp.float32
        )

    @pl.when(key_first > row_last)
    def _skip():
        l_out[...] = l_ref[...]
        acc_out[...] = acc_ref[...]

    @pl.when(key_last <= row_first)
    def _full():
        update(False)

    @pl.when(jnp.logical_and(key_first <= row_last, key_last > row_first))
    def _diagonal():
        update(True)


def attend_kernel(scalars, q, block, total, summed):
    n_q, hd = q.shape
    n_k = block.shape[1]
    tq = min(TQ, n_q)
    row = lambda i, sc: (i, 0)
    grid_spec = pltpu.PrefetchScalarGridSpec(
        num_scalar_prefetch=1,
        grid=(n_q // tq,),
        in_specs=[
            pl.BlockSpec((tq, hd), row),
            pl.BlockSpec((None, n_k, hd), lambda i, sc: (0, 0, 0)),
            pl.BlockSpec((None, n_k, hd), lambda i, sc: (1, 0, 0)),
            pl.BlockSpec((tq, 1), row),
            pl.BlockSpec((tq, hd), row),
        ],
        out_specs=[
            pl.BlockSpec((tq, 1), row),
            pl.BlockSpec((tq, hd), row),
        ],
    )
    return pl.pallas_call(
        block_kernel,
        grid_spec=grid_spec,
        out_shape=(
            jax.ShapeDtypeStruct(total.shape, jnp.float32),
            jax.ShapeDtypeStruct(summed.shape, jnp.float32),
        ),
        input_output_aliases={4: 0, 5: 1},
        cost_estimate=pl.CostEstimate(
            flops=4 * n_q * n_k * hd,
            transcendentals=2 * n_q * n_k,
            bytes_accessed=2 * (n_q + 2 * n_k) * hd + 8 * n_q * (hd + 1),
        ),
    )(scalars, q, block, block, total, summed)


def by_heads(queries, keys, values, row_first):
    n_kv = lax.axis_size(KV)
    me = lax.axis_index(KV)
    group = HQ // KVH
    rows_dev = queries.shape[0]
    key_dev = keys.shape[0]
    kv_local = keys.shape[1] // (n_kv * HD)
    kv_feat = kv_local * HD
    n_q = kv_local * group * rows_dev
    q_block = queries.reshape(rows_dev, kv_local * group, HD).transpose(1, 0, 2).reshape(n_q, HD)
    total = jnp.zeros((n_q, 1), jnp.float32)
    summed = jnp.zeros((n_q, HD), jnp.float32)
    for shift in range(n_kv):
        dest = me ^ shift
        src = dest
        block = jnp.stack(
            (
                lax.dynamic_slice_in_dim(keys, dest * kv_feat, kv_feat, 1),
                lax.dynamic_slice_in_dim(values, dest * kv_feat, kv_feat, 1),
            ),
            axis=0,
        )
        if shift:
            block = lax.ppermute(block, KV, [(j, j ^ shift) for j in range(n_kv)])
        scalars = jnp.stack([row_first, src * key_dev, jnp.int32(rows_dev)]).astype(jnp.int32)
        total, summed = attend_kernel(scalars, q_block, block, total, summed)
    mixed = (summed / total).astype(jnp.bfloat16)
    return mixed.reshape(kv_local * group, rows_dev, HD).transpose(1, 0, 2).reshape(rows_dev, n_q // rows_dev * HD)


def per_device(slab_start, queries, keys, values, out_weight):
    rows_dev = queries.shape[0]
    row_first = slab_start[0] + lax.axis_index("pb") * rows_dev
    attended = by_heads(queries, keys, values, row_first)
    partial = jnp.dot(attended, out_weight, preferred_element_type=jnp.float32)
    n_chip = lax.axis_size("kx")
    n_core = lax.axis_size("kc")
    partial = partial.reshape(n_chip, n_core, rows_dev // (n_chip * n_core), partial.shape[1])
    core = lax.axis_index("kc")
    mine = lax.dynamic_index_in_dim(partial, core, 1, keepdims=False)
    theirs = lax.dynamic_index_in_dim(partial, 1 - core, 1, keepdims=False)
    on_chip = mine + lax.ppermute(theirs, "kc", [(0, 1), (1, 0)])
    parts = lax.all_to_all(
        on_chip.astype(jnp.bfloat16), "kx", split_axis=0, concat_axis=0, tiled=True
    )
    return jnp.sum(parts.astype(jnp.float32), axis=0)


def solution(mesh):
    n_pb, n_kv = mesh.devices.shape
    split = Mesh(mesh.devices.reshape(n_pb, n_kv // 2, 2), ("pb", "kx", "kc"))
    in_specs = (P(), P("pb", KV), P(KV, None), P(KV, None), P(KV, None))
    out_specs = P(("pb",) + KV, None)
    return jax.shard_map(
        per_device, mesh=split, in_specs=in_specs, out_specs=out_specs, check_vma=False
    )
```

```python
import jax
import jax.numpy as jnp
from jax import lax
from jax.experimental import pallas as pl
from jax.experimental.pallas import tpu as pltpu
from jax.sharding import Mesh, PartitionSpec as P

HQ = 32
KVH = 16
HD = 128
CAP = 50
SCALAR = 144
KV = ("kx", "kc")
TQ = 256


def block_kernel(sc_ref, q_ref, k_ref, v_ref, l_ref, acc_ref, l_out, acc_out):
    tq = q_ref.shape[0]
    tk = k_ref.shape[0]
    row_first = sc_ref[0] + (pl.program_id(0) * tq) % sc_ref[2]
    row_last = row_first + tq - 1
    key_first = sc_ref[1]
    key_last = key_first + tk - 1

    def update(masked):
        raw = lax.dot_general(
            q_ref[...], k_ref[...], (((1,), (1,)), ((), ())), preferred_element_type=jnp.float32
        )
        prob = jnp.exp(CAP * jnp.tanh(raw * (SCALAR ** (-0.5) / CAP)))
        if masked:
            q_pos = row_first + lax.broadcasted_iota(jnp.int32, (tq, tk), 0)
            k_pos = key_first + lax.broadcasted_iota(jnp.int32, (tq, tk), 1)
            prob = jnp.where(k_pos <= q_pos, prob, 0.0)
        l_out[...] = l_ref[...] + jnp.sum(prob, axis=1, keepdims=True)
        acc_out[...] = acc_ref[...] + jnp.dot(
            prob.astype(jnp.bfloat16), v_ref[...], preferred_element_type=jnp.float32
        )

    @pl.when(key_first > row_last)
    def _skip():
        l_out[...] = l_ref[...]
        acc_out[...] = acc_ref[...]

    @pl.when(key_last <= row_first)
    def _full():
        update(False)

    @pl.when(jnp.logical_and(key_first <= row_last, key_last > row_first))
    def _diagonal():
        update(True)


def attend_kernel(scalars, q, block, total, summed):
    n_q, hd = q.shape
    n_k = block.shape[1]
    tq = min(TQ, n_q)
    row = lambda i, sc: (i, 0)
    grid_spec = pltpu.PrefetchScalarGridSpec(
        num_scalar_prefetch=1,
        grid=(n_q // tq,),
        in_specs=[
            pl.BlockSpec((tq, hd), row),
            pl.BlockSpec((None, n_k, hd), lambda i, sc: (0, 0, 0)),
            pl.BlockSpec((None, n_k, hd), lambda i, sc: (1, 0, 0)),
            pl.BlockSpec((tq, 1), row),
            pl.BlockSpec((tq, hd), row),
        ],
        out_specs=[
            pl.BlockSpec((tq, 1), row),
            pl.BlockSpec((tq, hd), row),
        ],
    )
    return pl.pallas_call(
        block_kernel,
        grid_spec=grid_spec,
        out_shape=(
            jax.ShapeDtypeStruct(total.shape, jnp.float32),
            jax.ShapeDtypeStruct(summed.shape, jnp.float32),
        ),
        input_output_aliases={4: 0, 5: 1},
        cost_estimate=pl.CostEstimate(
            flops=4 * n_q * n_k * hd,
            transcendentals=2 * n_q * n_k,
            bytes_accessed=2 * (n_q + 2 * n_k) * hd + 8 * n_q * (hd + 1),
        ),
    )(scalars, q, block, block, total, summed)


def by_heads(queries, keys, values, row_first):
    n_kv = lax.axis_size(KV)
    me = lax.axis_index(KV)
    group = HQ // KVH
    rows_dev = queries.shape[0]
    key_dev = keys.shape[0]
    kv_local = keys.shape[1] // (n_kv * HD)
    kv_feat = kv_local * HD
    n_q = kv_local * group * rows_dev
    q_block = queries.reshape(rows_dev, kv_local * group, HD).transpose(1, 0, 2).reshape(n_q, HD)
    total = jnp.zeros((n_q, 1), jnp.float32)
    summed = jnp.zeros((n_q, HD), jnp.float32)
    for shift in range(n_kv):
        dest = me ^ shift
        src = dest
        block = jnp.stack(
            (
                lax.dynamic_slice_in_dim(keys, dest * kv_feat, kv_feat, 1),
                lax.dynamic_slice_in_dim(values, dest * kv_feat, kv_feat, 1),
            ),
            axis=0,
        )
        if shift:
            block = lax.ppermute(block, KV, [(j, j ^ shift) for j in range(n_kv)])
        scalars = jnp.stack([row_first, src * key_dev, jnp.int32(rows_dev)]).astype(jnp.int32)
        total, summed = attend_kernel(scalars, q_block, block, total, summed)
    mixed = (summed / total).astype(jnp.bfloat16)
    return mixed.reshape(kv_local * group, rows_dev, HD).transpose(1, 0, 2).reshape(rows_dev, n_q // rows_dev * HD)


def per_device(slab_start, queries, keys, values, out_weight):
    rows_dev = queries.shape[0]
    row_first = slab_start[0] + lax.axis_index("pb") * rows_dev
    attended = by_heads(queries, keys, values, row_first)
    partial = jnp.dot(attended, out_weight, preferred_element_type=jnp.float32)
    n_chip = lax.axis_size("kx")
    n_core = lax.axis_size("kc")
    partial = partial.reshape(n_chip, n_core, rows_dev // (n_chip * n_core), partial.shape[1])
    core = lax.axis_index("kc")
    mine = lax.dynamic_index_in_dim(partial, core, 1, keepdims=False)
    theirs = lax.dynamic_index_in_dim(partial, 1 - core, 1, keepdims=False)
    on_chip = mine + lax.ppermute(theirs, "kc", [(0, 1), (1, 0)])
    chip = lax.axis_index("kx")
    result = lax.dynamic_index_in_dim(on_chip, chip, 0, keepdims=False)
    for mask in range(1, n_chip):
        part = lax.dynamic_index_in_dim(on_chip, chip ^ mask, 0, keepdims=False)
        moved = lax.ppermute(part.astype(jnp.bfloat16), "kx", [(k, k ^ mask) for k in range(n_chip)])
        result = result + moved.astype(jnp.float32)
    return result


def solution(mesh):
    n_pb, n_kv = mesh.devices.shape
    split = Mesh(mesh.devices.reshape(n_pb, n_kv // 2, 2), ("pb", "kx", "kc"))
    in_specs = (P(), P("pb", KV), P(KV, None), P(KV, None), P(KV, None))
    out_specs = P(("pb",) + KV, None)
    return jax.shard_map(
        per_device, mesh=split, in_specs=in_specs, out_specs=out_specs, check_vma=False
    )
```

```python
import functools

import jax
import jax.numpy as jnp
from jax import lax
from jax.experimental import pallas as pl
from jax.experimental.pallas import tpu as pltpu
from jax.sharding import Mesh, PartitionSpec as P

HQ = 32
KVH = 16
HD = 128
CAP = 50
SCALAR = 144
KV = ("kx", "kc")
TQ = 256


def block_kernel(sc_ref, q_ref, k_ref, v_ref, l_ref, acc_ref, l_out, acc_out, *, slot, rows):
    tq = q_ref.shape[0]
    tk = k_ref.shape[0]
    row_first = sc_ref[0] + (pl.program_id(0) * tq) % rows
    row_last = row_first + tq - 1
    key_first = sc_ref[1 + slot]
    key_last = key_first + tk - 1

    def update(masked):
        raw = lax.dot_general(
            q_ref[...], k_ref[...], (((1,), (1,)), ((), ())), preferred_element_type=jnp.float32
        )
        prob = jnp.exp(CAP * jnp.tanh(raw * (SCALAR ** (-0.5) / CAP)))
        if masked:
            q_pos = row_first + lax.broadcasted_iota(jnp.int32, (tq, tk), 0)
            k_pos = key_first + lax.broadcasted_iota(jnp.int32, (tq, tk), 1)
            prob = jnp.where(k_pos <= q_pos, prob, 0.0)
        l_out[...] = l_ref[...] + jnp.sum(prob, axis=1, keepdims=True)
        acc_out[...] = acc_ref[...] + jnp.dot(
            prob.astype(jnp.bfloat16), v_ref[...], preferred_element_type=jnp.float32
        )

    @pl.when(key_first > row_last)
    def _skip():
        l_out[...] = l_ref[...]
        acc_out[...] = acc_ref[...]

    @pl.when(key_last <= row_first)
    def _full():
        update(False)

    @pl.when(jnp.logical_and(key_first <= row_last, key_last > row_first))
    def _diagonal():
        update(True)


def attend_kernel(scalars, slot, rows, q, block, total, summed):
    n_q, hd = q.shape
    n_k = block.shape[1]
    tq = min(TQ, n_q)
    row = lambda i, sc: (i, 0)
    grid_spec = pltpu.PrefetchScalarGridSpec(
        num_scalar_prefetch=1,
        grid=(n_q // tq,),
        in_specs=[
            pl.BlockSpec((tq, hd), row),
            pl.BlockSpec((None, n_k, hd), lambda i, sc: (0, 0, 0)),
            pl.BlockSpec((None, n_k, hd), lambda i, sc: (1, 0, 0)),
            pl.BlockSpec((tq, 1), row),
            pl.BlockSpec((tq, hd), row),
        ],
        out_specs=[
            pl.BlockSpec((tq, 1), row),
            pl.BlockSpec((tq, hd), row),
        ],
    )
    return pl.pallas_call(
        functools.partial(block_kernel, slot=slot, rows=rows),
        grid_spec=grid_spec,
        out_shape=(
            jax.ShapeDtypeStruct(total.shape, jnp.float32),
            jax.ShapeDtypeStruct(summed.shape, jnp.float32),
        ),
        input_output_aliases={4: 0, 5: 1},
        cost_estimate=pl.CostEstimate(
            flops=4 * n_q * n_k * hd,
            transcendentals=2 * n_q * n_k,
            bytes_accessed=2 * (n_q + 2 * n_k) * hd + 8 * n_q * (hd + 1),
        ),
    )(scalars, q, block, block, total, summed)


def by_heads(queries, keys, values, row_first):
    n_kv = lax.axis_size(KV)
    me = lax.axis_index(KV)
    group = HQ // KVH
    rows_dev = queries.shape[0]
    key_dev = keys.shape[0]
    kv_local = keys.shape[1] // (n_kv * HD)
    kv_feat = kv_local * HD
    n_q = kv_local * group * rows_dev
    q_block = queries.reshape(rows_dev, kv_local * group, HD).transpose(1, 0, 2).reshape(n_q, HD)
    total = jnp.zeros((n_q, 1), jnp.float32)
    summed = jnp.zeros((n_q, HD), jnp.float32)
    table = jnp.stack(
        (keys.reshape(key_dev, n_kv, kv_feat), values.reshape(key_dev, n_kv, kv_feat)), axis=0
    ).transpose(2, 0, 1, 3)
    sources = me ^ jnp.arange(n_kv, dtype=jnp.int32)
    scalars = jnp.concatenate([row_first[None], sources * key_dev]).astype(jnp.int32)
    for shift in range(n_kv):
        block = lax.dynamic_index_in_dim(table, me ^ shift, 0, keepdims=False)
        if shift:
            block = lax.ppermute(block, KV, [(j, j ^ shift) for j in range(n_kv)])
        block = block.reshape(2, key_dev, kv_feat)
        total, summed = attend_kernel(scalars, shift, rows_dev, q_block, block, total, summed)
    mixed = (summed / total).astype(jnp.bfloat16)
    return mixed.reshape(kv_local * group, rows_dev, HD).transpose(1, 0, 2).reshape(rows_dev, n_q // rows_dev * HD)


def per_device(slab_start, queries, keys, values, out_weight):
    rows_dev = queries.shape[0]
    row_first = slab_start[0] + lax.axis_index("pb") * rows_dev
    attended = by_heads(queries, keys, values, row_first)
    partial = jnp.dot(attended, out_weight, preferred_element_type=jnp.float32)
    n_chip = lax.axis_size("kx")
    n_core = lax.axis_size("kc")
    partial = partial.reshape(n_chip, n_core, rows_dev // (n_chip * n_core), partial.shape[1])
    core = lax.axis_index("kc")
    mine = lax.dynamic_index_in_dim(partial, core, 1, keepdims=False)
    theirs = lax.dynamic_index_in_dim(partial, 1 - core, 1, keepdims=False)
    on_chip = mine + lax.ppermute(theirs, "kc", [(0, 1), (1, 0)])
    parts = lax.all_to_all(
        on_chip.astype(jnp.bfloat16), "kx", split_axis=0, concat_axis=0, tiled=True
    )
    return jnp.sum(parts.astype(jnp.float32), axis=0)


def solution(mesh):
    n_pb, n_kv = mesh.devices.shape
    split = Mesh(mesh.devices.reshape(n_pb, n_kv // 2, 2), ("pb", "kx", "kc"))
    in_specs = (P(), P("pb", KV), P(KV, None), P(KV, None), P(KV, None))
    out_specs = P(("pb",) + KV, None)
    return jax.shard_map(
        per_device, mesh=split, in_specs=in_specs, out_specs=out_specs, check_vma=False
    )
```

```python
import functools

import jax
import jax.numpy as jnp
from jax import lax
from jax.experimental import pallas as pl
from jax.experimental.pallas import tpu as pltpu
from jax.sharding import Mesh, PartitionSpec as P

HQ = 32
KVH = 16
HD = 128
CAP = 50
SCALAR = 144
KV = ("kx", "kc")
HALVES = 2
PER_CALL = 2
TQ = 256


def block_kernel(*refs, slots, run, stride, half):
    sc_ref, q_ref = refs[:2]
    kv_refs = refs[2 : 2 + 2 * len(slots)]
    l_ref, acc_ref, l_out, acc_out = refs[2 + 2 * len(slots) :]
    tq = q_ref.shape[0]
    row_first = sc_ref[0] + half * run
    row_last = row_first + (tq // run - 1) * stride + run - 1
    l_out[...] = l_ref[...]
    acc_out[...] = acc_ref[...]
    for number, slot in enumerate(slots):
        k_ref, v_ref = kv_refs[2 * number : 2 * number + 2]
        tk = k_ref.shape[0]
        key_first = sc_ref[1 + slot]
        key_last = key_first + tk - 1

        def update(masked, k_ref=k_ref, v_ref=v_ref, key_first=key_first, tk=tk):
            raw = lax.dot_general(
                q_ref[...], k_ref[...], (((1,), (1,)), ((), ())), preferred_element_type=jnp.float32
            )
            prob = jnp.exp(CAP * jnp.tanh(raw * (SCALAR ** (-0.5) / CAP)))
            if masked:
                rows = lax.broadcasted_iota(jnp.int32, (tq, tk), 0)
                shift = run.bit_length() - 1
                q_pos = row_first + lax.shift_right_logical(rows, shift) * stride + (rows & (run - 1))
                k_pos = key_first + lax.broadcasted_iota(jnp.int32, (tq, tk), 1)
                prob = jnp.where(k_pos <= q_pos, prob, 0.0)
            l_out[...] += jnp.sum(prob, axis=1, keepdims=True)
            acc_out[...] += jnp.dot(
                prob.astype(jnp.bfloat16), v_ref[...], preferred_element_type=jnp.float32
            )

        pl.when(key_last <= row_first)(lambda: update(False))
        pl.when(jnp.logical_and(key_first <= row_last, key_last > row_first))(
            lambda: update(True)
        )


def attend_kernel(scalars, slots, blocks, q, total, summed, run, stride, half, tq):
    n_q, hd = q.shape
    n_k = blocks[0].shape[1]
    row = lambda i, sc: (i, 0)
    kv_specs = []
    operands = []
    for block in blocks:
        kv_specs += [
            pl.BlockSpec((None, n_k, hd), lambda i, sc: (0, 0, 0)),
            pl.BlockSpec((None, n_k, hd), lambda i, sc: (1, 0, 0)),
        ]
        operands += [block, block]
    n_in = 2 + len(operands)
    grid_spec = pltpu.PrefetchScalarGridSpec(
        num_scalar_prefetch=1,
        grid=(n_q // tq,),
        in_specs=[pl.BlockSpec((tq, hd), row)]
        + kv_specs
        + [pl.BlockSpec((tq, 1), row), pl.BlockSpec((tq, hd), row)],
        out_specs=[pl.BlockSpec((tq, 1), row), pl.BlockSpec((tq, hd), row)],
    )
    n_keys = n_k * len(blocks)
    return pl.pallas_call(
        functools.partial(block_kernel, slots=slots, run=run, stride=stride, half=half),
        grid_spec=grid_spec,
        out_shape=(
            jax.ShapeDtypeStruct(total.shape, jnp.float32),
            jax.ShapeDtypeStruct(summed.shape, jnp.float32),
        ),
        input_output_aliases={n_in: 0, n_in + 1: 1},
        cost_estimate=pl.CostEstimate(
            flops=4 * n_q * n_keys * hd,
            transcendentals=2 * n_q * n_keys,
            bytes_accessed=2 * (n_q + 2 * n_keys) * hd + 8 * n_q * (hd + 1),
        ),
    )(scalars, q, *operands, total, summed)


def on_chip_sum(partial):
    n_chip = lax.axis_size("kx")
    n_core = lax.axis_size("kc")
    partial = partial.reshape(n_chip, n_core, -1, partial.shape[1])
    core = lax.axis_index("kc")
    mine = lax.dynamic_index_in_dim(partial, core, 1, keepdims=False)
    theirs = lax.dynamic_index_in_dim(partial, 1 - core, 1, keepdims=False)
    return mine + lax.ppermute(theirs, "kc", [(0, 1), (1, 0)])


def reduce_pieces(partial):
    n_chip = lax.axis_size("kx")
    on_chip = on_chip_sum(partial)
    chip = lax.axis_index("kx")
    pieces = [lax.dynamic_index_in_dim(on_chip, chip, 0, keepdims=False)]
    for mask in range(1, n_chip):
        part = lax.dynamic_index_in_dim(on_chip, chip ^ mask, 0, keepdims=False)
        pieces.append(
            lax.ppermute(part.astype(jnp.bfloat16), "kx", [(k, k ^ mask) for k in range(n_chip)])
        )
    return pieces


def add_pieces(pieces):
    result = pieces[0]
    for piece in pieces[1:]:
        result = result + piece.astype(jnp.float32)
    return result


def reduce_all(partial):
    parts = lax.all_to_all(
        on_chip_sum(partial).astype(jnp.bfloat16), "kx", split_axis=0, concat_axis=0, tiled=True
    )
    return jnp.sum(parts.astype(jnp.float32), axis=0)


def per_device(slab_start, queries, keys, values, out_weight):
    n_kv = lax.axis_size(KV)
    me = lax.axis_index(KV)
    group = HQ // KVH
    rows_dev = queries.shape[0]
    row_first = slab_start[0] + lax.axis_index("pb") * rows_dev
    key_dev = keys.shape[0]
    kv_local = keys.shape[1] // (n_kv * HD)
    kv_feat = kv_local * HD
    heads = kv_local * group
    chunk = rows_dev // n_kv
    run = chunk // HALVES
    q_halves = (
        queries.reshape(n_kv, HALVES, run, heads, HD)
        .transpose(1, 3, 0, 2, 4)
        .reshape(HALVES, heads * n_kv * run, HD)
    )
    n_q = heads * n_kv * run
    tq = n_kv * run
    table = jnp.stack(
        (keys.reshape(key_dev, n_kv, kv_feat), values.reshape(key_dev, n_kv, kv_feat)), axis=0
    ).transpose(2, 0, 1, 3)
    sources = me ^ jnp.arange(n_kv, dtype=jnp.int32)
    scalars = jnp.concatenate([row_first[None], sources * key_dev]).astype(jnp.int32)
    blocks = []
    for shift in range(n_kv):
        block = lax.dynamic_index_in_dim(table, me ^ shift, 0, keepdims=False)
        if shift:
            block = lax.ppermute(block, KV, [(j, j ^ shift) for j in range(n_kv)])
        blocks.append(block.reshape(2, key_dev, kv_feat))
    results = []
    pending = []
    for half in range(HALVES):
        total = jnp.zeros((n_q, 1), jnp.float32)
        summed = jnp.zeros((n_q, HD), jnp.float32)
        for call in range(0, n_kv, PER_CALL):
            at = call // PER_CALL
            if at < len(pending):
                pending[at], total = lax.optimization_barrier((pending[at], total))
            slots = tuple(range(call, call + PER_CALL))
            total, summed = attend_kernel(
                scalars, slots, [blocks[s] for s in slots], q_halves[half], total, summed,
                run, chunk, half, tq,
            )
        if pending:
            results.append(add_pieces(pending))
        mixed = (summed / total).astype(jnp.bfloat16)
        attended = (
            mixed.reshape(heads, n_kv * run, HD).transpose(1, 0, 2).reshape(n_kv * run, heads * HD)
        )
        partial = jnp.dot(attended, out_weight, preferred_element_type=jnp.float32)
        if half + 1 < HALVES:
            pending = reduce_pieces(partial)
        else:
            results.append(reduce_all(partial))
    return jnp.concatenate(results, axis=0)


def solution(mesh):
    n_pb, n_kv = mesh.devices.shape
    split = Mesh(mesh.devices.reshape(n_pb, n_kv // 2, 2), ("pb", "kx", "kc"))
    in_specs = (P(), P("pb", KV), P(KV, None), P(KV, None), P(KV, None))
    out_specs = P(("pb",) + KV, None)
    return jax.shard_map(
        per_device, mesh=split, in_specs=in_specs, out_specs=out_specs, check_vma=False
    )
```

```python
import jax
import jax.numpy as jnp
from jax import lax
from jax.experimental import pallas as pl
from jax.experimental.pallas import tpu as pltpu
from jax.sharding import Mesh, PartitionSpec as P

HQ = 32
KVH = 16
HD = 128
CAP = 50
SCALAR = 144
KV = ("kx", "kc")
TQ = 256


def block_kernel(sc_ref, q_ref, k_ref, v_ref, l_ref, acc_ref, l_out, acc_out):
    tq = q_ref.shape[0]
    tk = k_ref.shape[0]
    row_first = sc_ref[0] + (pl.program_id(0) * tq) % sc_ref[2]
    row_last = row_first + tq - 1
    key_first = sc_ref[1]
    key_last = key_first + tk - 1

    def update(masked):
        raw = lax.dot_general(
            q_ref[...], k_ref[...], (((1,), (1,)), ((), ())), preferred_element_type=jnp.float32
        )
        prob = jnp.exp(CAP * jnp.tanh(raw * (SCALAR ** (-0.5) / CAP)))
        if masked:
            q_pos = row_first + lax.broadcasted_iota(jnp.int32, (tq, tk), 0)
            k_pos = key_first + lax.broadcasted_iota(jnp.int32, (tq, tk), 1)
            prob = jnp.where(k_pos <= q_pos, prob, 0.0)
        l_out[...] = l_ref[...] + jnp.sum(prob, axis=1, keepdims=True)
        acc_out[...] = acc_ref[...] + jnp.dot(
            prob.astype(jnp.bfloat16), v_ref[...], preferred_element_type=jnp.float32
        )

    @pl.when(key_first > row_last)
    def _skip():
        l_out[...] = l_ref[...]
        acc_out[...] = acc_ref[...]

    @pl.when(key_last <= row_first)
    def _full():
        update(False)

    @pl.when(jnp.logical_and(key_first <= row_last, key_last > row_first))
    def _diagonal():
        update(True)


def attend_kernel(scalars, q, block, total, summed):
    n_q, hd = q.shape
    n_k = block.shape[1]
    tq = min(TQ, n_q)
    row = lambda i, sc: (i, 0)
    grid_spec = pltpu.PrefetchScalarGridSpec(
        num_scalar_prefetch=1,
        grid=(n_q // tq,),
        in_specs=[
            pl.BlockSpec((tq, hd), row),
            pl.BlockSpec((None, n_k, hd), lambda i, sc: (0, 0, 0)),
            pl.BlockSpec((None, n_k, hd), lambda i, sc: (1, 0, 0)),
            pl.BlockSpec((tq, 1), row),
            pl.BlockSpec((tq, hd), row),
        ],
        out_specs=[
            pl.BlockSpec((tq, 1), row),
            pl.BlockSpec((tq, hd), row),
        ],
    )
    return pl.pallas_call(
        block_kernel,
        grid_spec=grid_spec,
        out_shape=(
            jax.ShapeDtypeStruct(total.shape, jnp.float32),
            jax.ShapeDtypeStruct(summed.shape, jnp.float32),
        ),
        input_output_aliases={4: 0, 5: 1},
        cost_estimate=pl.CostEstimate(
            flops=4 * n_q * n_k * hd,
            transcendentals=2 * n_q * n_k,
            bytes_accessed=2 * (n_q + 2 * n_k) * hd + 8 * n_q * (hd + 1),
        ),
    )(scalars, q, block, block, total, summed)


def by_heads(queries, keys, values, row_first):
    n_kv = lax.axis_size(KV)
    me = lax.axis_index(KV)
    group = HQ // KVH
    rows_dev = queries.shape[0]
    key_dev = keys.shape[0]
    kv_local = keys.shape[1] // (n_kv * HD)
    kv_feat = kv_local * HD
    n_q = kv_local * group * rows_dev
    q_block = queries.reshape(rows_dev, kv_local * group, HD).transpose(1, 0, 2).reshape(n_q, HD)
    total = jnp.zeros((n_q, 1), jnp.float32)
    summed = jnp.zeros((n_q, HD), jnp.float32)
    for shift in range(n_kv):
        dest = me ^ shift
        src = dest
        block = jnp.stack(
            (
                lax.dynamic_slice_in_dim(keys, dest * kv_feat, kv_feat, 1),
                lax.dynamic_slice_in_dim(values, dest * kv_feat, kv_feat, 1),
            ),
            axis=0,
        )
        if shift:
            block = lax.ppermute(block, KV, [(j, j ^ shift) for j in range(n_kv)])
        scalars = jnp.stack([row_first, src * key_dev, jnp.int32(rows_dev)]).astype(jnp.int32)
        total, summed = attend_kernel(scalars, q_block, block, total, summed)
    mixed = (summed / total).astype(jnp.bfloat16)
    return mixed.reshape(kv_local * group, rows_dev, HD).transpose(1, 0, 2).reshape(rows_dev, n_q // rows_dev * HD)


def per_device(slab_start, queries, keys, values, out_weight):
    rows_dev = queries.shape[0]
    row_first = slab_start[0] + lax.axis_index("pb") * rows_dev
    attended = by_heads(queries, keys, values, row_first)
    partial = jnp.dot(attended, out_weight, preferred_element_type=jnp.float32)
    n_chip = lax.axis_size("kx")
    n_core = lax.axis_size("kc")
    partial = partial.reshape(n_chip, n_core, rows_dev // (n_chip * n_core), partial.shape[1])
    core = lax.axis_index("kc")
    mine = lax.dynamic_index_in_dim(partial, core, 1, keepdims=False)
    theirs = lax.dynamic_index_in_dim(partial, 1 - core, 1, keepdims=False).astype(jnp.bfloat16)
    on_chip = mine + lax.ppermute(theirs, "kc", [(0, 1), (1, 0)]).astype(jnp.float32)
    parts = lax.all_to_all(
        on_chip.astype(jnp.bfloat16), "kx", split_axis=0, concat_axis=0, tiled=True
    )
    return jnp.sum(parts.astype(jnp.float32), axis=0)


def solution(mesh):
    n_pb, n_kv = mesh.devices.shape
    split = Mesh(mesh.devices.reshape(n_pb, n_kv // 2, 2), ("pb", "kx", "kc"))
    in_specs = (P(), P("pb", KV), P(KV, None), P(KV, None), P(KV, None))
    out_specs = P(("pb",) + KV, None)
    return jax.shard_map(
        per_device, mesh=split, in_specs=in_specs, out_specs=out_specs, check_vma=False
    )
```

```python
import jax
import jax.numpy as jnp
from jax import lax
from jax.experimental import pallas as pl
from jax.experimental.pallas import tpu as pltpu
from jax.sharding import Mesh, PartitionSpec as P

HQ = 32
KVH = 16
HD = 128
CAP = 50
SCALAR = 144
KV = ("kx", "kc")
TQ = 256


def block_kernel(sc_ref, q_ref, k_ref, v_ref, l_ref, acc_ref, l_out, acc_out):
    tq = q_ref.shape[0]
    tk = k_ref.shape[0]
    row_first = sc_ref[0] + (pl.program_id(0) * tq) % sc_ref[2]
    row_last = row_first + tq - 1
    key_first = sc_ref[1]
    key_last = key_first + tk - 1

    def update(masked):
        raw = lax.dot_general(
            q_ref[...], k_ref[...], (((1,), (1,)), ((), ())), preferred_element_type=jnp.float32
        )
        prob = jnp.exp(CAP * jnp.tanh(raw * (SCALAR ** (-0.5) / CAP)))
        if masked:
            q_pos = row_first + lax.broadcasted_iota(jnp.int32, (tq, tk), 0)
            k_pos = key_first + lax.broadcasted_iota(jnp.int32, (tq, tk), 1)
            prob = jnp.where(k_pos <= q_pos, prob, 0.0)
        l_out[...] = l_ref[...] + jnp.sum(prob, axis=1, keepdims=True)
        acc_out[...] = acc_ref[...] + jnp.dot(
            prob.astype(jnp.bfloat16), v_ref[...], preferred_element_type=jnp.float32
        )

    @pl.when(key_first > row_last)
    def _skip():
        l_out[...] = l_ref[...]
        acc_out[...] = acc_ref[...]

    @pl.when(key_last <= row_first)
    def _full():
        update(False)

    @pl.when(jnp.logical_and(key_first <= row_last, key_last > row_first))
    def _diagonal():
        update(True)


def attend_kernel(scalars, q, block, total, summed):
    n_q, hd = q.shape
    n_k = block.shape[1]
    tq = min(TQ, n_q)
    row = lambda i, sc: (i, 0)
    grid_spec = pltpu.PrefetchScalarGridSpec(
        num_scalar_prefetch=1,
        grid=(n_q // tq,),
        in_specs=[
            pl.BlockSpec((tq, hd), row),
            pl.BlockSpec((None, n_k, hd), lambda i, sc: (0, 0, 0)),
            pl.BlockSpec((None, n_k, hd), lambda i, sc: (1, 0, 0)),
            pl.BlockSpec((tq, 1), row),
            pl.BlockSpec((tq, hd), row),
        ],
        out_specs=[
            pl.BlockSpec((tq, 1), row),
            pl.BlockSpec((tq, hd), row),
        ],
    )
    return pl.pallas_call(
        block_kernel,
        grid_spec=grid_spec,
        out_shape=(
            jax.ShapeDtypeStruct(total.shape, jnp.float32),
            jax.ShapeDtypeStruct(summed.shape, jnp.float32),
        ),
        input_output_aliases={4: 0, 5: 1},
        cost_estimate=pl.CostEstimate(
            flops=4 * n_q * n_k * hd,
            transcendentals=2 * n_q * n_k,
            bytes_accessed=2 * (n_q + 2 * n_k) * hd + 8 * n_q * (hd + 1),
        ),
    )(scalars, q, block, block, total, summed)


def by_heads(queries, keys, values, row_first):
    n_kv = lax.axis_size(KV)
    me = lax.axis_index(KV)
    group = HQ // KVH
    rows_dev = queries.shape[0]
    key_dev = keys.shape[0]
    kv_local = keys.shape[1] // (n_kv * HD)
    kv_feat = kv_local * HD
    n_q = kv_local * group * rows_dev
    q_block = queries.reshape(rows_dev, kv_local * group, HD).transpose(1, 0, 2).reshape(n_q, HD)
    total = jnp.zeros((n_q, 1), jnp.float32)
    summed = jnp.zeros((n_q, HD), jnp.float32)
    for shift in range(n_kv):
        dest = me ^ shift
        src = dest
        block = jnp.stack(
            (
                lax.dynamic_slice_in_dim(keys, dest * kv_feat, kv_feat, 1),
                lax.dynamic_slice_in_dim(values, dest * kv_feat, kv_feat, 1),
            ),
            axis=0,
        )
        if shift:
            block = lax.ppermute(block, KV, [(j, j ^ shift) for j in range(n_kv)])
        scalars = jnp.stack([row_first, src * key_dev, jnp.int32(rows_dev)]).astype(jnp.int32)
        total, summed = attend_kernel(scalars, q_block, block, total, summed)
    mixed = (summed / total).astype(jnp.bfloat16)
    return mixed.reshape(kv_local * group, rows_dev, HD).transpose(1, 0, 2).reshape(rows_dev, n_q // rows_dev * HD)


def per_device(slab_start, queries, keys, values, out_weight):
    rows_dev = queries.shape[0]
    row_first = slab_start[0] + lax.axis_index("pb") * rows_dev
    attended = by_heads(queries, keys, values, row_first)
    partial = jnp.dot(attended, out_weight, preferred_element_type=jnp.float32)
    n_chip = lax.axis_size("kx")
    n_core = lax.axis_size("kc")
    partial = partial.reshape(n_chip, n_core, rows_dev // (n_chip * n_core), partial.shape[1])
    core = lax.axis_index("kc")
    mine = lax.dynamic_index_in_dim(partial, core, 1, keepdims=False)
    theirs = lax.dynamic_index_in_dim(partial, 1 - core, 1, keepdims=False).astype(jnp.bfloat16)
    on_chip = mine + lax.ppermute(theirs, "kc", [(0, 1), (1, 0)]).astype(jnp.float32)
    return lax.psum_scatter(
        on_chip.astype(jnp.bfloat16), "kx", scatter_dimension=0, tiled=True
    ).reshape(on_chip.shape[1:]).astype(jnp.float32)


def solution(mesh):
    n_pb, n_kv = mesh.devices.shape
    split = Mesh(mesh.devices.reshape(n_pb, n_kv // 2, 2), ("pb", "kx", "kc"))
    in_specs = (P(), P("pb", KV), P(KV, None), P(KV, None), P(KV, None))
    out_specs = P(("pb",) + KV, None)
    return jax.shard_map(
        per_device, mesh=split, in_specs=in_specs, out_specs=out_specs, check_vma=False
    )
```

```python
import jax
import jax.numpy as jnp
from jax import lax
from jax.experimental import pallas as pl
from jax.experimental.pallas import tpu as pltpu
from jax.sharding import Mesh, PartitionSpec as P

HQ = 32
KVH = 16
HD = 128
CAP = 50
SCALAR = 144
KV = ("kx", "kc")
TQ = 256


def block_kernel(sc_ref, q_ref, k_ref, v_ref, l_ref, acc_ref, l_out, acc_out):
    tq = q_ref.shape[0]
    tk = k_ref.shape[0]
    row_first = sc_ref[0] + (pl.program_id(0) * tq) % sc_ref[2]
    row_last = row_first + tq - 1
    key_first = sc_ref[1]
    key_last = key_first + tk - 1

    def update(masked):
        raw = lax.dot_general(
            q_ref[...], k_ref[...], (((1,), (1,)), ((), ())), preferred_element_type=jnp.float32
        )
        prob = jnp.exp(CAP * jnp.tanh(raw * (SCALAR ** (-0.5) / CAP)))
        if masked:
            q_pos = row_first + lax.broadcasted_iota(jnp.int32, (tq, tk), 0)
            k_pos = key_first + lax.broadcasted_iota(jnp.int32, (tq, tk), 1)
            prob = jnp.where(k_pos <= q_pos, prob, 0.0)
        weights = prob.astype(jnp.bfloat16)
        ones = jnp.ones((tk, v_ref.shape[1]), jnp.bfloat16)
        sums = jnp.dot(weights, ones, preferred_element_type=jnp.float32)
        l_out[...] = l_ref[...] + sums[:, :1]
        acc_out[...] = acc_ref[...] + jnp.dot(
            weights, v_ref[...], preferred_element_type=jnp.float32
        )

    @pl.when(key_first > row_last)
    def _skip():
        l_out[...] = l_ref[...]
        acc_out[...] = acc_ref[...]

    @pl.when(key_last <= row_first)
    def _full():
        update(False)

    @pl.when(jnp.logical_and(key_first <= row_last, key_last > row_first))
    def _diagonal():
        update(True)


def attend_kernel(scalars, q, block, total, summed):
    n_q, hd = q.shape
    n_k = block.shape[1]
    tq = min(TQ, n_q)
    row = lambda i, sc: (i, 0)
    grid_spec = pltpu.PrefetchScalarGridSpec(
        num_scalar_prefetch=1,
        grid=(n_q // tq,),
        in_specs=[
            pl.BlockSpec((tq, hd), row),
            pl.BlockSpec((None, n_k, hd), lambda i, sc: (0, 0, 0)),
            pl.BlockSpec((None, n_k, hd), lambda i, sc: (1, 0, 0)),
            pl.BlockSpec((tq, 1), row),
            pl.BlockSpec((tq, hd), row),
        ],
        out_specs=[
            pl.BlockSpec((tq, 1), row),
            pl.BlockSpec((tq, hd), row),
        ],
    )
    return pl.pallas_call(
        block_kernel,
        grid_spec=grid_spec,
        out_shape=(
            jax.ShapeDtypeStruct(total.shape, jnp.float32),
            jax.ShapeDtypeStruct(summed.shape, jnp.float32),
        ),
        input_output_aliases={4: 0, 5: 1},
        cost_estimate=pl.CostEstimate(
            flops=4 * n_q * n_k * hd,
            transcendentals=2 * n_q * n_k,
            bytes_accessed=2 * (n_q + 2 * n_k) * hd + 8 * n_q * (hd + 1),
        ),
    )(scalars, q, block, block, total, summed)


def by_heads(queries, keys, values, row_first):
    n_kv = lax.axis_size(KV)
    me = lax.axis_index(KV)
    group = HQ // KVH
    rows_dev = queries.shape[0]
    key_dev = keys.shape[0]
    kv_local = keys.shape[1] // (n_kv * HD)
    kv_feat = kv_local * HD
    n_q = kv_local * group * rows_dev
    q_block = queries.reshape(rows_dev, kv_local * group, HD).transpose(1, 0, 2).reshape(n_q, HD)
    total = jnp.zeros((n_q, 1), jnp.float32)
    summed = jnp.zeros((n_q, HD), jnp.float32)
    for shift in range(n_kv):
        dest = me ^ shift
        src = dest
        block = jnp.stack(
            (
                lax.dynamic_slice_in_dim(keys, dest * kv_feat, kv_feat, 1),
                lax.dynamic_slice_in_dim(values, dest * kv_feat, kv_feat, 1),
            ),
            axis=0,
        )
        if shift:
            block = lax.ppermute(block, KV, [(j, j ^ shift) for j in range(n_kv)])
        scalars = jnp.stack([row_first, src * key_dev, jnp.int32(rows_dev)]).astype(jnp.int32)
        total, summed = attend_kernel(scalars, q_block, block, total, summed)
    mixed = (summed / total).astype(jnp.bfloat16)
    return mixed.reshape(kv_local * group, rows_dev, HD).transpose(1, 0, 2).reshape(rows_dev, n_q // rows_dev * HD)


def per_device(slab_start, queries, keys, values, out_weight):
    rows_dev = queries.shape[0]
    row_first = slab_start[0] + lax.axis_index("pb") * rows_dev
    attended = by_heads(queries, keys, values, row_first)
    partial = jnp.dot(attended, out_weight, preferred_element_type=jnp.float32)
    n_chip = lax.axis_size("kx")
    n_core = lax.axis_size("kc")
    partial = partial.reshape(n_chip, n_core, rows_dev // (n_chip * n_core), partial.shape[1])
    core = lax.axis_index("kc")
    mine = lax.dynamic_index_in_dim(partial, core, 1, keepdims=False)
    theirs = lax.dynamic_index_in_dim(partial, 1 - core, 1, keepdims=False)
    on_chip = mine + lax.ppermute(theirs, "kc", [(0, 1), (1, 0)])
    parts = lax.all_to_all(
        on_chip.astype(jnp.bfloat16), "kx", split_axis=0, concat_axis=0, tiled=True
    )
    return jnp.sum(parts.astype(jnp.float32), axis=0)


def solution(mesh):
    n_pb, n_kv = mesh.devices.shape
    split = Mesh(mesh.devices.reshape(n_pb, n_kv // 2, 2), ("pb", "kx", "kc"))
    in_specs = (P(), P("pb", KV), P(KV, None), P(KV, None), P(KV, None))
    out_specs = P(("pb",) + KV, None)
    return jax.shard_map(
        per_device, mesh=split, in_specs=in_specs, out_specs=out_specs, check_vma=False
    )
```

```python
import jax
import jax.numpy as jnp
from jax import lax
from jax.experimental import pallas as pl
from jax.experimental.pallas import tpu as pltpu
from jax.sharding import Mesh, PartitionSpec as P

HQ = 32
KVH = 16
HD = 128
CAP = 50
SCALAR = 144
KV = ("kx", "kc")
TQ = 256


def block_kernel(sc_ref, q_ref, k_ref, v_ref, l_ref, acc_ref, l_out, acc_out):
    tq = q_ref.shape[0]
    tk = k_ref.shape[0]
    row_first = sc_ref[0] + (pl.program_id(0) * tq) % sc_ref[2]
    row_last = row_first + tq - 1
    key_first = sc_ref[1]
    key_last = key_first + tk - 1

    def update(masked):
        raw = lax.dot_general(
            q_ref[...], k_ref[...], (((1,), (1,)), ((), ())), preferred_element_type=jnp.float32
        )
        prob = jnp.exp(CAP * jnp.tanh(raw * (SCALAR ** (-0.5) / CAP)))
        if masked:
            q_pos = row_first + lax.broadcasted_iota(jnp.int32, (tq, tk), 0)
            k_pos = key_first + lax.broadcasted_iota(jnp.int32, (tq, tk), 1)
            prob = jnp.where(k_pos <= q_pos, prob, 0.0)
        l_out[...] = l_ref[...] + jnp.sum(prob, axis=1, keepdims=True)
        acc_out[...] = acc_ref[...] + jnp.dot(
            prob.astype(jnp.bfloat16), v_ref[...], preferred_element_type=jnp.float32
        )

    @pl.when(key_first > row_last)
    def _skip():
        l_out[...] = l_ref[...]
        acc_out[...] = acc_ref[...]

    @pl.when(key_last <= row_first)
    def _full():
        update(False)

    @pl.when(jnp.logical_and(key_first <= row_last, key_last > row_first))
    def _diagonal():
        update(True)


def attend_kernel(scalars, q, block, total, summed):
    n_q, hd = q.shape
    n_k = block.shape[1]
    tq = min(TQ, n_q)
    row = lambda i, sc: (i, 0)
    grid_spec = pltpu.PrefetchScalarGridSpec(
        num_scalar_prefetch=1,
        grid=(n_q // tq,),
        in_specs=[
            pl.BlockSpec((tq, hd), row),
            pl.BlockSpec((None, n_k, hd), lambda i, sc: (0, 0, 0)),
            pl.BlockSpec((None, n_k, hd), lambda i, sc: (1, 0, 0)),
            pl.BlockSpec((tq, 1), row),
            pl.BlockSpec((tq, hd), row),
        ],
        out_specs=[
            pl.BlockSpec((tq, 1), row),
            pl.BlockSpec((tq, hd), row),
        ],
    )
    return pl.pallas_call(
        block_kernel,
        grid_spec=grid_spec,
        out_shape=(
            jax.ShapeDtypeStruct(total.shape, jnp.float32),
            jax.ShapeDtypeStruct(summed.shape, jnp.float32),
        ),
        input_output_aliases={4: 0, 5: 1},
        cost_estimate=pl.CostEstimate(
            flops=4 * n_q * n_k * hd,
            transcendentals=2 * n_q * n_k,
            bytes_accessed=2 * (n_q + 2 * n_k) * hd + 8 * n_q * (hd + 1),
        ),
    )(scalars, q, block, block, total, summed)


def by_heads(queries, keys, values, row_first):
    n_kv = lax.axis_size(KV)
    me = lax.axis_index(KV)
    group = HQ // KVH
    rows_dev = queries.shape[0]
    key_dev = keys.shape[0]
    kv_local = keys.shape[1] // (n_kv * HD)
    kv_feat = kv_local * HD
    n_q = kv_local * group * rows_dev
    q_block = queries.reshape(rows_dev, kv_local * group, HD).transpose(1, 0, 2).reshape(n_q, HD)
    total = jnp.zeros((n_q, 1), jnp.float32)
    summed = jnp.zeros((n_q, HD), jnp.float32)
    for shift in range(n_kv):
        dest = me ^ shift
        src = dest
        block = jnp.stack(
            (
                lax.dynamic_slice_in_dim(keys, dest * kv_feat, kv_feat, 1),
                lax.dynamic_slice_in_dim(values, dest * kv_feat, kv_feat, 1),
            ),
            axis=0,
        )
        if shift:
            block = lax.ppermute(block, KV, [(j, j ^ shift) for j in range(n_kv)])
        scalars = jnp.stack([row_first, src * key_dev, jnp.int32(rows_dev)]).astype(jnp.int32)
        total, summed = attend_kernel(scalars, q_block, block, total, summed)
    mixed = (summed / total).astype(jnp.bfloat16)
    return mixed.reshape(kv_local * group, rows_dev, HD).transpose(1, 0, 2).reshape(rows_dev, n_q // rows_dev * HD)


def per_device(slab_start, queries, keys, values, out_weight):
    rows_dev = queries.shape[0]
    row_first = slab_start[0] + lax.axis_index("pb") * rows_dev
    attended = by_heads(queries, keys, values, row_first)
    n_chip = lax.axis_size("kx")
    n_core = lax.axis_size("kc")
    by_core = attended.reshape(n_chip, n_core, rows_dev // (n_chip * n_core), attended.shape[1])
    core = lax.axis_index("kc")

    def project(which):
        rows = lax.dynamic_index_in_dim(by_core, which, 1, keepdims=False)
        return jnp.einsum("cra,ad->crd", rows, out_weight, preferred_element_type=jnp.float32)

    theirs = project(1 - core)
    moved = lax.ppermute(theirs, "kc", [(0, 1), (1, 0)])
    on_chip = project(core) + moved
    parts = lax.all_to_all(
        on_chip.astype(jnp.bfloat16), "kx", split_axis=0, concat_axis=0, tiled=True
    )
    return jnp.sum(parts.astype(jnp.float32), axis=0)


def solution(mesh):
    n_pb, n_kv = mesh.devices.shape
    split = Mesh(mesh.devices.reshape(n_pb, n_kv // 2, 2), ("pb", "kx", "kc"))
    in_specs = (P(), P("pb", KV), P(KV, None), P(KV, None), P(KV, None))
    out_specs = P(("pb",) + KV, None)
    return jax.shard_map(
        per_device, mesh=split, in_specs=in_specs, out_specs=out_specs, check_vma=False
    )
```

```python
import jax
import jax.numpy as jnp
from jax import lax
from jax.experimental import pallas as pl
from jax.experimental.pallas import tpu as pltpu
from jax.sharding import Mesh, PartitionSpec as P

HQ = 32
KVH = 16
HD = 128
CAP = 50
SCALAR = 144
KV = ("kx", "kc")
TQ = 256


def block_kernel(sc_ref, q_ref, k_ref, v_ref, l_ref, acc_ref, l_out, acc_out):
    tq = q_ref.shape[0]
    tk = k_ref.shape[0]
    row_first = sc_ref[0] + (pl.program_id(0) * tq) % sc_ref[2]
    row_last = row_first + tq - 1
    key_first = sc_ref[1]
    key_last = key_first + tk - 1

    def update(masked):
        raw = lax.dot_general(
            q_ref[...], k_ref[...], (((1,), (1,)), ((), ())), preferred_element_type=jnp.float32
        )
        prob = jnp.exp(CAP * jnp.tanh(raw * (SCALAR ** (-0.5) / CAP)))
        if masked:
            q_pos = row_first + lax.broadcasted_iota(jnp.int32, (tq, tk), 0)
            k_pos = key_first + lax.broadcasted_iota(jnp.int32, (tq, tk), 1)
            prob = jnp.where(k_pos <= q_pos, prob, 0.0)
        l_out[...] = l_ref[...] + jnp.sum(prob, axis=1, keepdims=True)
        acc_out[...] = acc_ref[...] + jnp.dot(
            prob.astype(jnp.bfloat16), v_ref[...], preferred_element_type=jnp.float32
        )

    @pl.when(key_first > row_last)
    def _skip():
        l_out[...] = l_ref[...]
        acc_out[...] = acc_ref[...]

    @pl.when(key_last <= row_first)
    def _full():
        update(False)

    @pl.when(jnp.logical_and(key_first <= row_last, key_last > row_first))
    def _diagonal():
        update(True)


def attend_kernel(scalars, q, key_part, value_part, total, summed):
    n_q, hd = q.shape
    n_k = key_part.shape[0]
    tq = min(TQ, n_q)
    row = lambda i, sc: (i, 0)
    grid_spec = pltpu.PrefetchScalarGridSpec(
        num_scalar_prefetch=1,
        grid=(n_q // tq,),
        in_specs=[
            pl.BlockSpec((tq, hd), row),
            pl.BlockSpec((n_k, hd), lambda i, sc: (0, 0)),
            pl.BlockSpec((n_k, hd), lambda i, sc: (0, 0)),
            pl.BlockSpec((tq, 1), row),
            pl.BlockSpec((tq, hd), row),
        ],
        out_specs=[
            pl.BlockSpec((tq, 1), row),
            pl.BlockSpec((tq, hd), row),
        ],
    )
    return pl.pallas_call(
        block_kernel,
        grid_spec=grid_spec,
        out_shape=(
            jax.ShapeDtypeStruct(total.shape, jnp.float32),
            jax.ShapeDtypeStruct(summed.shape, jnp.float32),
        ),
        input_output_aliases={4: 0, 5: 1},
        cost_estimate=pl.CostEstimate(
            flops=4 * n_q * n_k * hd,
            transcendentals=2 * n_q * n_k,
            bytes_accessed=2 * (n_q + 2 * n_k) * hd + 8 * n_q * (hd + 1),
        ),
    )(scalars, q, key_part, value_part, total, summed)


def by_heads(queries, keys, values, row_first):
    n_kv = lax.axis_size(KV)
    me = lax.axis_index(KV)
    group = HQ // KVH
    rows_dev = queries.shape[0]
    key_dev = keys.shape[0]
    kv_local = keys.shape[1] // (n_kv * HD)
    kv_feat = kv_local * HD
    n_q = kv_local * group * rows_dev
    q_block = queries.reshape(rows_dev, kv_local * group, HD).transpose(1, 0, 2).reshape(n_q, HD)
    total = jnp.zeros((n_q, 1), jnp.float32)
    summed = jnp.zeros((n_q, HD), jnp.float32)
    for shift in range(n_kv):
        dest = me ^ shift
        src = dest
        block = (
            lax.dynamic_slice_in_dim(keys, dest * kv_feat, kv_feat, 1),
            lax.dynamic_slice_in_dim(values, dest * kv_feat, kv_feat, 1),
        )
        if shift:
            block = lax.ppermute(block, KV, [(j, j ^ shift) for j in range(n_kv)])
        scalars = jnp.stack([row_first, src * key_dev, jnp.int32(rows_dev)]).astype(jnp.int32)
        total, summed = attend_kernel(scalars, q_block, *block, total, summed)
    mixed = (summed / total).astype(jnp.bfloat16)
    return mixed.reshape(kv_local * group, rows_dev, HD).transpose(1, 0, 2).reshape(rows_dev, n_q // rows_dev * HD)


def per_device(slab_start, queries, keys, values, out_weight):
    rows_dev = queries.shape[0]
    row_first = slab_start[0] + lax.axis_index("pb") * rows_dev
    attended = by_heads(queries, keys, values, row_first)
    partial = jnp.dot(attended, out_weight, preferred_element_type=jnp.float32)
    n_chip = lax.axis_size("kx")
    n_core = lax.axis_size("kc")
    partial = partial.reshape(n_chip, n_core, rows_dev // (n_chip * n_core), partial.shape[1])
    core = lax.axis_index("kc")
    mine = lax.dynamic_index_in_dim(partial, core, 1, keepdims=False)
    theirs = lax.dynamic_index_in_dim(partial, 1 - core, 1, keepdims=False)
    on_chip = mine + lax.ppermute(theirs, "kc", [(0, 1), (1, 0)])
    parts = lax.all_to_all(
        on_chip.astype(jnp.bfloat16), "kx", split_axis=0, concat_axis=0, tiled=True
    )
    return jnp.sum(parts.astype(jnp.float32), axis=0)


def solution(mesh):
    n_pb, n_kv = mesh.devices.shape
    split = Mesh(mesh.devices.reshape(n_pb, n_kv // 2, 2), ("pb", "kx", "kc"))
    in_specs = (P(), P("pb", KV), P(KV, None), P(KV, None), P(KV, None))
    out_specs = P(("pb",) + KV, None)
    return jax.shard_map(
        per_device, mesh=split, in_specs=in_specs, out_specs=out_specs, check_vma=False
    )
```

```python
import jax
import jax.numpy as jnp
from jax import lax
from jax.experimental import pallas as pl
from jax.experimental.pallas import tpu as pltpu
from jax.sharding import Mesh, PartitionSpec as P

HQ = 32
KVH = 16
HD = 128
CAP = 50
SCALAR = 144
KV = ("kx", "kc")
TQ = 256
LAG = 4


def block_kernel(sc_ref, q_ref, k_ref, v_ref, l_ref, acc_ref, l_out, acc_out):
    tq = q_ref.shape[0]
    tk = k_ref.shape[0]
    row_first = sc_ref[0] + (pl.program_id(0) * tq) % sc_ref[2]
    row_last = row_first + tq - 1
    key_first = sc_ref[1]
    key_last = key_first + tk - 1

    def update(masked):
        raw = lax.dot_general(
            q_ref[...], k_ref[...], (((1,), (1,)), ((), ())), preferred_element_type=jnp.float32
        )
        prob = jnp.exp(CAP * jnp.tanh(raw * (SCALAR ** (-0.5) / CAP)))
        if masked:
            q_pos = row_first + lax.broadcasted_iota(jnp.int32, (tq, tk), 0)
            k_pos = key_first + lax.broadcasted_iota(jnp.int32, (tq, tk), 1)
            prob = jnp.where(k_pos <= q_pos, prob, 0.0)
        l_out[...] = l_ref[...] + jnp.sum(prob, axis=1, keepdims=True)
        acc_out[...] = acc_ref[...] + jnp.dot(
            prob.astype(jnp.bfloat16), v_ref[...], preferred_element_type=jnp.float32
        )

    @pl.when(key_first > row_last)
    def _skip():
        l_out[...] = l_ref[...]
        acc_out[...] = acc_ref[...]

    @pl.when(key_last <= row_first)
    def _full():
        update(False)

    @pl.when(jnp.logical_and(key_first <= row_last, key_last > row_first))
    def _diagonal():
        update(True)


def attend_kernel(scalars, q, block, total, summed):
    n_q, hd = q.shape
    n_k = block.shape[1]
    tq = min(TQ, n_q)
    row = lambda i, sc: (i, 0)
    grid_spec = pltpu.PrefetchScalarGridSpec(
        num_scalar_prefetch=1,
        grid=(n_q // tq,),
        in_specs=[
            pl.BlockSpec((tq, hd), row),
            pl.BlockSpec((None, n_k, hd), lambda i, sc: (0, 0, 0)),
            pl.BlockSpec((None, n_k, hd), lambda i, sc: (1, 0, 0)),
            pl.BlockSpec((tq, 1), row),
            pl.BlockSpec((tq, hd), row),
        ],
        out_specs=[
            pl.BlockSpec((tq, 1), row),
            pl.BlockSpec((tq, hd), row),
        ],
    )
    return pl.pallas_call(
        block_kernel,
        grid_spec=grid_spec,
        out_shape=(
            jax.ShapeDtypeStruct(total.shape, jnp.float32),
            jax.ShapeDtypeStruct(summed.shape, jnp.float32),
        ),
        input_output_aliases={4: 0, 5: 1},
        cost_estimate=pl.CostEstimate(
            flops=4 * n_q * n_k * hd,
            transcendentals=2 * n_q * n_k,
            bytes_accessed=2 * (n_q + 2 * n_k) * hd + 8 * n_q * (hd + 1),
        ),
    )(scalars, q, block, block, total, summed)


def by_heads(queries, keys, values, row_first):
    n_kv = lax.axis_size(KV)
    me = lax.axis_index(KV)
    group = HQ // KVH
    rows_dev = queries.shape[0]
    key_dev = keys.shape[0]
    kv_local = keys.shape[1] // (n_kv * HD)
    kv_feat = kv_local * HD
    n_q = kv_local * group * rows_dev
    q_block = queries.reshape(rows_dev, kv_local * group, HD).transpose(1, 0, 2).reshape(n_q, HD)
    total = jnp.zeros((n_q, 1), jnp.float32)
    summed = jnp.zeros((n_q, HD), jnp.float32)
    sends = []
    for shift in range(n_kv):
        dest = me ^ shift
        sends.append(
            jnp.stack(
                (
                    lax.dynamic_slice_in_dim(keys, dest * kv_feat, kv_feat, 1),
                    lax.dynamic_slice_in_dim(values, dest * kv_feat, kv_feat, 1),
                ),
                axis=0,
            )
        )
    received = [sends[0]]
    for shift in range(1, min(LAG + 1, n_kv)):
        received.append(lax.ppermute(sends[shift], KV, [(j, j ^ shift) for j in range(n_kv)]))
    for shift in range(n_kv):
        src = me ^ shift
        scalars = jnp.stack([row_first, src * key_dev, jnp.int32(rows_dev)]).astype(jnp.int32)
        total, summed = attend_kernel(scalars, q_block, received[shift], total, summed)
        nxt = shift + LAG + 1
        if nxt < n_kv:
            payload, total = lax.optimization_barrier((sends[nxt], total))
            received.append(lax.ppermute(payload, KV, [(j, j ^ nxt) for j in range(n_kv)]))
    mixed = (summed / total).astype(jnp.bfloat16)
    return mixed.reshape(kv_local * group, rows_dev, HD).transpose(1, 0, 2).reshape(rows_dev, n_q // rows_dev * HD)


def per_device(slab_start, queries, keys, values, out_weight):
    rows_dev = queries.shape[0]
    row_first = slab_start[0] + lax.axis_index("pb") * rows_dev
    attended = by_heads(queries, keys, values, row_first)
    partial = jnp.dot(attended, out_weight, preferred_element_type=jnp.float32)
    n_chip = lax.axis_size("kx")
    n_core = lax.axis_size("kc")
    partial = partial.reshape(n_chip, n_core, rows_dev // (n_chip * n_core), partial.shape[1])
    core = lax.axis_index("kc")
    mine = lax.dynamic_index_in_dim(partial, core, 1, keepdims=False)
    theirs = lax.dynamic_index_in_dim(partial, 1 - core, 1, keepdims=False)
    on_chip = mine + lax.ppermute(theirs, "kc", [(0, 1), (1, 0)])
    parts = lax.all_to_all(
        on_chip.astype(jnp.bfloat16), "kx", split_axis=0, concat_axis=0, tiled=True
    )
    return jnp.sum(parts.astype(jnp.float32), axis=0)


def solution(mesh):
    n_pb, n_kv = mesh.devices.shape
    split = Mesh(mesh.devices.reshape(n_pb, n_kv // 2, 2), ("pb", "kx", "kc"))
    in_specs = (P(), P("pb", KV), P(KV, None), P(KV, None), P(KV, None))
    out_specs = P(("pb",) + KV, None)
    return jax.shard_map(
        per_device, mesh=split, in_specs=in_specs, out_specs=out_specs, check_vma=False
    )
```

```python
import jax
import jax.numpy as jnp
from jax import lax
from jax.experimental import pallas as pl
from jax.experimental.pallas import tpu as pltpu
from jax.sharding import Mesh, PartitionSpec as P

HQ = 32
KVH = 16
HD = 128
CAP = 50
SCALAR = 144
KV = ("kx", "kc")
TQ = 256


def block_kernel(sc_ref, q_ref, k_ref, v_ref, l_ref, acc_ref, l_out, acc_out):
    tq = q_ref.shape[0]
    tk = k_ref.shape[0]
    row_first = sc_ref[0] + (pl.program_id(0) * tq) % sc_ref[2]
    row_last = row_first + tq - 1
    key_first = sc_ref[1]
    key_last = key_first + tk - 1

    def update(masked):
        raw = lax.dot_general(
            q_ref[...], k_ref[...], (((1,), (1,)), ((), ())), preferred_element_type=jnp.float32
        )
        prob = jnp.exp(CAP * jnp.tanh(raw * (SCALAR ** (-0.5) / CAP)))
        if masked:
            q_pos = row_first + lax.broadcasted_iota(jnp.int32, (tq, tk), 0)
            k_pos = key_first + lax.broadcasted_iota(jnp.int32, (tq, tk), 1)
            prob = jnp.where(k_pos <= q_pos, prob, 0.0)
        l_out[...] = l_ref[...] + jnp.sum(prob, axis=1, keepdims=True)
        acc_out[...] = acc_ref[...] + jnp.dot(
            prob.astype(jnp.bfloat16), v_ref[...], preferred_element_type=jnp.float32
        )

    @pl.when(key_first > row_last)
    def _skip():
        l_out[...] = l_ref[...]
        acc_out[...] = acc_ref[...]

    @pl.when(key_last <= row_first)
    def _full():
        update(False)

    @pl.when(jnp.logical_and(key_first <= row_last, key_last > row_first))
    def _diagonal():
        update(True)


def attend_kernel(scalars, q, block, total, summed):
    n_q, hd = q.shape
    n_k = block.shape[1]
    tq = min(TQ, n_q)
    row = lambda i, sc: (i, 0)
    grid_spec = pltpu.PrefetchScalarGridSpec(
        num_scalar_prefetch=1,
        grid=(n_q // tq,),
        in_specs=[
            pl.BlockSpec((tq, hd), row),
            pl.BlockSpec((None, n_k, hd), lambda i, sc: (0, 0, 0)),
            pl.BlockSpec((None, n_k, hd), lambda i, sc: (1, 0, 0)),
            pl.BlockSpec((tq, 1), row),
            pl.BlockSpec((tq, hd), row),
        ],
        out_specs=[
            pl.BlockSpec((tq, 1), row),
            pl.BlockSpec((tq, hd), row),
        ],
    )
    return pl.pallas_call(
        block_kernel,
        grid_spec=grid_spec,
        out_shape=(
            jax.ShapeDtypeStruct(total.shape, jnp.float32),
            jax.ShapeDtypeStruct(summed.shape, jnp.float32),
        ),
        input_output_aliases={4: 0, 5: 1},
        cost_estimate=pl.CostEstimate(
            flops=4 * n_q * n_k * hd,
            transcendentals=2 * n_q * n_k,
            bytes_accessed=2 * (n_q + 2 * n_k) * hd + 8 * n_q * (hd + 1),
        ),
    )(scalars, q, block, block, total, summed)


def by_heads(queries, keys, values, row_first):
    n_kv = lax.axis_size(KV)
    me = lax.axis_index(KV)
    group = HQ // KVH
    rows_dev = queries.shape[0]
    key_dev = keys.shape[0]
    kv_local = keys.shape[1] // (n_kv * HD)
    kv_feat = kv_local * HD
    n_q = kv_local * group * rows_dev
    q_block = queries.reshape(rows_dev, kv_local * group, HD).transpose(1, 0, 2).reshape(n_q, HD)
    total = jnp.zeros((n_q, 1), jnp.float32)
    summed = jnp.zeros((n_q, HD), jnp.float32)
    for shift in range(n_kv):
        dest = me ^ shift
        src = dest
        block = jnp.stack(
            (
                lax.dynamic_slice_in_dim(keys, dest * kv_feat, kv_feat, 1),
                lax.dynamic_slice_in_dim(values, dest * kv_feat, kv_feat, 1),
            ),
            axis=0,
        )
        if shift & 2:
            n_pb = lax.axis_size("pb")
            pairs = [
                (p * n_kv + j, (p ^ 1) * n_kv + (j ^ shift)) for p in range(n_pb) for j in range(n_kv)
            ]
            block = lax.ppermute(block, ("pb",) + KV, pairs)
        elif shift:
            block = lax.ppermute(block, KV, [(j, j ^ shift) for j in range(n_kv)])
        scalars = jnp.stack([row_first, src * key_dev, jnp.int32(rows_dev)]).astype(jnp.int32)
        total, summed = attend_kernel(scalars, q_block, block, total, summed)
    mixed = (summed / total).astype(jnp.bfloat16)
    return mixed.reshape(kv_local * group, rows_dev, HD).transpose(1, 0, 2).reshape(rows_dev, n_q // rows_dev * HD)


def per_device(slab_start, queries, keys, values, out_weight):
    rows_dev = queries.shape[0]
    row_first = slab_start[0] + lax.axis_index("pb") * rows_dev
    attended = by_heads(queries, keys, values, row_first)
    partial = jnp.dot(attended, out_weight, preferred_element_type=jnp.float32)
    n_chip = lax.axis_size("kx")
    n_core = lax.axis_size("kc")
    partial = partial.reshape(n_chip, n_core, rows_dev // (n_chip * n_core), partial.shape[1])
    core = lax.axis_index("kc")
    mine = lax.dynamic_index_in_dim(partial, core, 1, keepdims=False)
    theirs = lax.dynamic_index_in_dim(partial, 1 - core, 1, keepdims=False)
    on_chip = mine + lax.ppermute(theirs, "kc", [(0, 1), (1, 0)])
    parts = lax.all_to_all(
        on_chip.astype(jnp.bfloat16), "kx", split_axis=0, concat_axis=0, tiled=True
    )
    return jnp.sum(parts.astype(jnp.float32), axis=0)


def solution(mesh):
    n_pb, n_kv = mesh.devices.shape
    split = Mesh(mesh.devices.reshape(n_pb, n_kv // 2, 2), ("pb", "kx", "kc"))
    in_specs = (P(), P("pb", KV), P(KV, None), P(KV, None), P(KV, None))
    out_specs = P(("pb",) + KV, None)
    return jax.shard_map(
        per_device, mesh=split, in_specs=in_specs, out_specs=out_specs, check_vma=False
    )
```

```python
import jax
import jax.numpy as jnp
from jax import lax
from jax.experimental import pallas as pl
from jax.experimental.pallas import tpu as pltpu
from jax.sharding import Mesh, PartitionSpec as P

HQ = 32
KVH = 16
HD = 128
CAP = 50
SCALAR = 144
CHIP = ("kxx", "kxy")
KV = CHIP + ("kc",)
TQ = 256


def block_kernel(sc_ref, q_ref, k_ref, v_ref, l_ref, acc_ref, l_out, acc_out):
    tq = q_ref.shape[0]
    tk = k_ref.shape[0]
    row_first = sc_ref[0] + (pl.program_id(0) * tq) % sc_ref[2]
    row_last = row_first + tq - 1
    key_first = sc_ref[1]
    key_last = key_first + tk - 1

    def update(masked):
        raw = lax.dot_general(
            q_ref[...], k_ref[...], (((1,), (1,)), ((), ())), preferred_element_type=jnp.float32
        )
        prob = jnp.exp(CAP * jnp.tanh(raw * (SCALAR ** (-0.5) / CAP)))
        if masked:
            q_pos = row_first + lax.broadcasted_iota(jnp.int32, (tq, tk), 0)
            k_pos = key_first + lax.broadcasted_iota(jnp.int32, (tq, tk), 1)
            prob = jnp.where(k_pos <= q_pos, prob, 0.0)
        l_out[...] = l_ref[...] + jnp.sum(prob, axis=1, keepdims=True)
        acc_out[...] = acc_ref[...] + jnp.dot(
            prob.astype(jnp.bfloat16), v_ref[...], preferred_element_type=jnp.float32
        )

    @pl.when(key_first > row_last)
    def _skip():
        l_out[...] = l_ref[...]
        acc_out[...] = acc_ref[...]

    @pl.when(key_last <= row_first)
    def _full():
        update(False)

    @pl.when(jnp.logical_and(key_first <= row_last, key_last > row_first))
    def _diagonal():
        update(True)


def attend_kernel(scalars, q, block, total, summed):
    n_q, hd = q.shape
    n_k = block.shape[1]
    tq = min(TQ, n_q)
    row = lambda i, sc: (i, 0)
    grid_spec = pltpu.PrefetchScalarGridSpec(
        num_scalar_prefetch=1,
        grid=(n_q // tq,),
        in_specs=[
            pl.BlockSpec((tq, hd), row),
            pl.BlockSpec((None, n_k, hd), lambda i, sc: (0, 0, 0)),
            pl.BlockSpec((None, n_k, hd), lambda i, sc: (1, 0, 0)),
            pl.BlockSpec((tq, 1), row),
            pl.BlockSpec((tq, hd), row),
        ],
        out_specs=[
            pl.BlockSpec((tq, 1), row),
            pl.BlockSpec((tq, hd), row),
        ],
    )
    return pl.pallas_call(
        block_kernel,
        grid_spec=grid_spec,
        out_shape=(
            jax.ShapeDtypeStruct(total.shape, jnp.float32),
            jax.ShapeDtypeStruct(summed.shape, jnp.float32),
        ),
        input_output_aliases={4: 0, 5: 1},
        cost_estimate=pl.CostEstimate(
            flops=4 * n_q * n_k * hd,
            transcendentals=2 * n_q * n_k,
            bytes_accessed=2 * (n_q + 2 * n_k) * hd + 8 * n_q * (hd + 1),
        ),
    )(scalars, q, block, block, total, summed)


def by_heads(queries, keys, values, row_first):
    n_kv = lax.axis_size(KV)
    me = lax.axis_index(KV)
    group = HQ // KVH
    rows_dev = queries.shape[0]
    key_dev = keys.shape[0]
    kv_local = keys.shape[1] // (n_kv * HD)
    kv_feat = kv_local * HD
    n_q = kv_local * group * rows_dev
    q_block = queries.reshape(rows_dev, kv_local * group, HD).transpose(1, 0, 2).reshape(n_q, HD)
    total = jnp.zeros((n_q, 1), jnp.float32)
    summed = jnp.zeros((n_q, HD), jnp.float32)
    for shift in range(n_kv):
        dest = me ^ shift
        src = dest
        block = jnp.stack(
            (
                lax.dynamic_slice_in_dim(keys, dest * kv_feat, kv_feat, 1),
                lax.dynamic_slice_in_dim(values, dest * kv_feat, kv_feat, 1),
            ),
            axis=0,
        )
        if shift:
            block = lax.ppermute(block, KV, [(j, j ^ shift) for j in range(n_kv)])
        scalars = jnp.stack([row_first, src * key_dev, jnp.int32(rows_dev)]).astype(jnp.int32)
        total, summed = attend_kernel(scalars, q_block, block, total, summed)
    mixed = (summed / total).astype(jnp.bfloat16)
    return mixed.reshape(kv_local * group, rows_dev, HD).transpose(1, 0, 2).reshape(rows_dev, n_q // rows_dev * HD)


def per_device(slab_start, queries, keys, values, out_weight):
    rows_dev = queries.shape[0]
    row_first = slab_start[0] + lax.axis_index("pb") * rows_dev
    attended = by_heads(queries, keys, values, row_first)
    partial = jnp.dot(attended, out_weight, preferred_element_type=jnp.float32)
    n_chip = lax.axis_size(CHIP)
    n_core = lax.axis_size("kc")
    partial = partial.reshape(n_chip, n_core, rows_dev // (n_chip * n_core), partial.shape[1])
    core = lax.axis_index("kc")
    mine = lax.dynamic_index_in_dim(partial, core, 1, keepdims=False)
    theirs = lax.dynamic_index_in_dim(partial, 1 - core, 1, keepdims=False)
    on_chip = mine + lax.ppermute(theirs, "kc", [(0, 1), (1, 0)])
    n_y = lax.axis_size("kxy")
    on_chip = on_chip.reshape(n_chip // n_y, n_y, *on_chip.shape[1:])
    y = lax.axis_index("kxy")
    near = lax.dynamic_index_in_dim(on_chip, y, 1, keepdims=False)
    far = lax.dynamic_index_in_dim(on_chip, 1 - y, 1, keepdims=False).astype(jnp.bfloat16)
    on_row = near + lax.ppermute(far, "kxy", [(0, 1), (1, 0)]).astype(jnp.float32)
    parts = lax.all_to_all(
        on_row.astype(jnp.bfloat16), "kxx", split_axis=0, concat_axis=0, tiled=True
    )
    return jnp.sum(parts.astype(jnp.float32), axis=0)


def solution(mesh):
    n_pb, n_kv = mesh.devices.shape
    split = Mesh(mesh.devices.reshape(n_pb, n_kv // 4, 2, 2), ("pb",) + KV)
    in_specs = (P(), P("pb", KV), P(KV, None), P(KV, None), P(KV, None))
    out_specs = P(("pb",) + KV, None)
    return jax.shard_map(
        per_device, mesh=split, in_specs=in_specs, out_specs=out_specs, check_vma=False
    )
```

```python
import functools

import jax
import jax.numpy as jnp
from jax import lax
from jax.experimental import pallas as pl
from jax.experimental.pallas import tpu as pltpu
from jax.sharding import Mesh, PartitionSpec as P

HQ = 32
KVH = 16
HD = 128
CAP = 50
SCALAR = 144
KV = ("kx", "kc")
TQ = 256


def block_kernel(sc_ref, q_ref, k_ref, v_ref, l_ref, acc_ref, l_out, acc_out, *, slot, rows):
    tq = q_ref.shape[0]
    tk = k_ref.shape[0]
    row_first = sc_ref[0] + (pl.program_id(0) * tq) % rows
    row_last = row_first + tq - 1
    key_first = sc_ref[1 + slot]
    key_last = key_first + tk - 1

    def update(masked):
        raw = lax.dot_general(
            q_ref[...], k_ref[...], (((1,), (1,)), ((), ())), preferred_element_type=jnp.float32
        )
        prob = jnp.exp(CAP * jnp.tanh(raw * (SCALAR ** (-0.5) / CAP)))
        if masked:
            q_pos = row_first + lax.broadcasted_iota(jnp.int32, (tq, tk), 0)
            k_pos = key_first + lax.broadcasted_iota(jnp.int32, (tq, tk), 1)
            prob = jnp.where(k_pos <= q_pos, prob, 0.0)
        l_out[...] = l_ref[...] + jnp.sum(prob, axis=1, keepdims=True)
        acc_out[...] = acc_ref[...] + jnp.dot(
            prob.astype(jnp.bfloat16), v_ref[...], preferred_element_type=jnp.float32
        )

    @pl.when(key_first > row_last)
    def _skip():
        l_out[...] = l_ref[...]
        acc_out[...] = acc_ref[...]

    @pl.when(key_last <= row_first)
    def _full():
        update(False)

    @pl.when(jnp.logical_and(key_first <= row_last, key_last > row_first))
    def _diagonal():
        update(True)


def attend_kernel(scalars, slot, rows, q, block, total, summed):
    n_q, hd = q.shape
    n_k = block.shape[1]
    tq = min(TQ, n_q)
    row = lambda i, sc: (i, 0)
    grid_spec = pltpu.PrefetchScalarGridSpec(
        num_scalar_prefetch=1,
        grid=(n_q // tq,),
        in_specs=[
            pl.BlockSpec((tq, hd), row),
            pl.BlockSpec((None, n_k, hd), lambda i, sc: (0, 0, 0)),
            pl.BlockSpec((None, n_k, hd), lambda i, sc: (1, 0, 0)),
            pl.BlockSpec((tq, 1), row),
            pl.BlockSpec((tq, hd), row),
        ],
        out_specs=[
            pl.BlockSpec((tq, 1), row),
            pl.BlockSpec((tq, hd), row),
        ],
    )
    return pl.pallas_call(
        functools.partial(block_kernel, slot=slot, rows=rows),
        grid_spec=grid_spec,
        out_shape=(
            jax.ShapeDtypeStruct(total.shape, jnp.float32),
            jax.ShapeDtypeStruct(summed.shape, jnp.float32),
        ),
        input_output_aliases={4: 0, 5: 1},
        cost_estimate=pl.CostEstimate(
            flops=4 * n_q * n_k * hd,
            transcendentals=2 * n_q * n_k,
            bytes_accessed=2 * (n_q + 2 * n_k) * hd + 8 * n_q * (hd + 1),
        ),
    )(scalars, q, block, block, total, summed)


def by_heads(queries, keys, values, row_first):
    n_kv = lax.axis_size(KV)
    me = lax.axis_index(KV)
    group = HQ // KVH
    rows_dev = queries.shape[0]
    key_dev = keys.shape[0]
    kv_local = keys.shape[1] // (n_kv * HD)
    kv_feat = kv_local * HD
    n_q = kv_local * group * rows_dev
    q_block = queries.reshape(rows_dev, kv_local * group, HD).transpose(1, 0, 2).reshape(n_q, HD)
    total = jnp.zeros((n_q, 1), jnp.float32)
    summed = jnp.zeros((n_q, HD), jnp.float32)
    sources = me ^ jnp.arange(n_kv, dtype=jnp.int32)
    scalars = jnp.concatenate([row_first[None], sources * key_dev]).astype(jnp.int32)
    for shift in range(n_kv):
        dest = me ^ shift
        src = dest
        block = jnp.stack(
            (
                lax.dynamic_slice_in_dim(keys, dest * kv_feat, kv_feat, 1),
                lax.dynamic_slice_in_dim(values, dest * kv_feat, kv_feat, 1),
            ),
            axis=0,
        )
        if shift:
            block = lax.ppermute(block, KV, [(j, j ^ shift) for j in range(n_kv)])
        total, summed = attend_kernel(scalars, shift, rows_dev, q_block, block, total, summed)
    mixed = (summed / total).astype(jnp.bfloat16)
    return mixed.reshape(kv_local * group, rows_dev, HD).transpose(1, 0, 2).reshape(rows_dev, n_q // rows_dev * HD)


def per_device(slab_start, queries, keys, values, out_weight):
    rows_dev = queries.shape[0]
    row_first = slab_start[0] + lax.axis_index("pb") * rows_dev
    attended = by_heads(queries, keys, values, row_first)
    partial = jnp.dot(attended, out_weight, preferred_element_type=jnp.float32)
    n_chip = lax.axis_size("kx")
    n_core = lax.axis_size("kc")
    partial = partial.reshape(n_chip, n_core, rows_dev // (n_chip * n_core), partial.shape[1])
    core = lax.axis_index("kc")
    mine = lax.dynamic_index_in_dim(partial, core, 1, keepdims=False)
    theirs = lax.dynamic_index_in_dim(partial, 1 - core, 1, keepdims=False)
    on_chip = mine + lax.ppermute(theirs, "kc", [(0, 1), (1, 0)])
    parts = lax.all_to_all(
        on_chip.astype(jnp.bfloat16), "kx", split_axis=0, concat_axis=0, tiled=True
    )
    return jnp.sum(parts.astype(jnp.float32), axis=0)


def solution(mesh):
    n_pb, n_kv = mesh.devices.shape
    split = Mesh(mesh.devices.reshape(n_pb, n_kv // 2, 2), ("pb", "kx", "kc"))
    in_specs = (P(), P("pb", KV), P(KV, None), P(KV, None), P(KV, None))
    out_specs = P(("pb",) + KV, None)
    return jax.shard_map(
        per_device, mesh=split, in_specs=in_specs, out_specs=out_specs, check_vma=False
    )
```

```python
import functools

import jax
import jax.numpy as jnp
from jax import lax
from jax.experimental import pallas as pl
from jax.experimental.pallas import tpu as pltpu
from jax.sharding import Mesh, PartitionSpec as P

HQ = 32
KVH = 16
HD = 128
CAP = 50
SCALAR = 144
KV = ("kx", "kc")
TQ = 512


def block_kernel(sc_ref, q_ref, k_ref, v_ref, l_ref, acc_ref, l_out, acc_out, *, slot, rows):
    tq = q_ref.shape[0]
    tk = k_ref.shape[0]
    row_first = sc_ref[0] + (pl.program_id(0) * tq) % rows
    row_last = row_first + tq - 1
    key_first = sc_ref[1 + slot]
    key_last = key_first + tk - 1

    def update(masked):
        raw = lax.dot_general(
            q_ref[...], k_ref[...], (((1,), (1,)), ((), ())), preferred_element_type=jnp.float32
        )
        prob = jnp.exp(CAP * jnp.tanh(raw * (SCALAR ** (-0.5) / CAP)))
        if masked:
            q_pos = row_first + lax.broadcasted_iota(jnp.int32, (tq, tk), 0)
            k_pos = key_first + lax.broadcasted_iota(jnp.int32, (tq, tk), 1)
            prob = jnp.where(k_pos <= q_pos, prob, 0.0)
        l_out[...] = l_ref[...] + jnp.sum(prob, axis=1, keepdims=True)
        acc_out[...] = acc_ref[...] + jnp.dot(
            prob.astype(jnp.bfloat16), v_ref[...], preferred_element_type=jnp.float32
        )

    @pl.when(key_first > row_last)
    def _skip():
        l_out[...] = l_ref[...]
        acc_out[...] = acc_ref[...]

    @pl.when(key_last <= row_first)
    def _full():
        update(False)

    @pl.when(jnp.logical_and(key_first <= row_last, key_last > row_first))
    def _diagonal():
        update(True)


def attend_kernel(scalars, slot, rows, q, block, total, summed):
    n_q, hd = q.shape
    n_k = block.shape[1]
    tq = min(TQ, n_q)
    row = lambda i, sc: (i, 0)
    grid_spec = pltpu.PrefetchScalarGridSpec(
        num_scalar_prefetch=1,
        grid=(n_q // tq,),
        in_specs=[
            pl.BlockSpec((tq, hd), row),
            pl.BlockSpec((None, n_k, hd), lambda i, sc: (0, 0, 0)),
            pl.BlockSpec((None, n_k, hd), lambda i, sc: (1, 0, 0)),
            pl.BlockSpec((tq, 1), row),
            pl.BlockSpec((tq, hd), row),
        ],
        out_specs=[
            pl.BlockSpec((tq, 1), row),
            pl.BlockSpec((tq, hd), row),
        ],
    )
    return pl.pallas_call(
        functools.partial(block_kernel, slot=slot, rows=rows),
        grid_spec=grid_spec,
        out_shape=(
            jax.ShapeDtypeStruct(total.shape, jnp.float32),
            jax.ShapeDtypeStruct(summed.shape, jnp.float32),
        ),
        input_output_aliases={4: 0, 5: 1},
        cost_estimate=pl.CostEstimate(
            flops=4 * n_q * n_k * hd,
            transcendentals=2 * n_q * n_k,
            bytes_accessed=2 * (n_q + 2 * n_k) * hd + 8 * n_q * (hd + 1),
        ),
    )(scalars, q, block, block, total, summed)


def by_heads(queries, keys, values, row_first):
    n_kv = lax.axis_size(KV)
    me = lax.axis_index(KV)
    group = HQ // KVH
    rows_dev = queries.shape[0]
    key_dev = keys.shape[0]
    kv_local = keys.shape[1] // (n_kv * HD)
    kv_feat = kv_local * HD
    n_q = kv_local * group * rows_dev
    q_block = queries.reshape(rows_dev, kv_local * group, HD).transpose(1, 0, 2).reshape(n_q, HD)
    total = jnp.zeros((n_q, 1), jnp.float32)
    summed = jnp.zeros((n_q, HD), jnp.float32)
    sources = me ^ jnp.arange(n_kv, dtype=jnp.int32)
    scalars = jnp.concatenate([row_first[None], sources * key_dev]).astype(jnp.int32)
    for shift in range(n_kv):
        dest = me ^ shift
        src = dest
        block = jnp.stack(
            (
                lax.dynamic_slice_in_dim(keys, dest * kv_feat, kv_feat, 1),
                lax.dynamic_slice_in_dim(values, dest * kv_feat, kv_feat, 1),
            ),
            axis=0,
        )
        if shift:
            block = lax.ppermute(block, KV, [(j, j ^ shift) for j in range(n_kv)])
        total, summed = attend_kernel(scalars, shift, rows_dev, q_block, block, total, summed)
    mixed = (summed / total).astype(jnp.bfloat16)
    return mixed.reshape(kv_local * group, rows_dev, HD).transpose(1, 0, 2).reshape(rows_dev, n_q // rows_dev * HD)


def per_device(slab_start, queries, keys, values, out_weight):
    rows_dev = queries.shape[0]
    row_first = slab_start[0] + lax.axis_index("pb") * rows_dev
    attended = by_heads(queries, keys, values, row_first)
    partial = jnp.dot(attended, out_weight, preferred_element_type=jnp.float32)
    n_chip = lax.axis_size("kx")
    n_core = lax.axis_size("kc")
    partial = partial.reshape(n_chip, n_core, rows_dev // (n_chip * n_core), partial.shape[1])
    core = lax.axis_index("kc")
    mine = lax.dynamic_index_in_dim(partial, core, 1, keepdims=False)
    theirs = lax.dynamic_index_in_dim(partial, 1 - core, 1, keepdims=False)
    on_chip = mine + lax.ppermute(theirs, "kc", [(0, 1), (1, 0)])
    parts = lax.all_to_all(
        on_chip.astype(jnp.bfloat16), "kx", split_axis=0, concat_axis=0, tiled=True
    )
    return jnp.sum(parts.astype(jnp.float32), axis=0)


def solution(mesh):
    n_pb, n_kv = mesh.devices.shape
    split = Mesh(mesh.devices.reshape(n_pb, n_kv // 2, 2), ("pb", "kx", "kc"))
    in_specs = (P(), P("pb", KV), P(KV, None), P(KV, None), P(KV, None))
    out_specs = P(("pb",) + KV, None)
    return jax.shard_map(
        per_device, mesh=split, in_specs=in_specs, out_specs=out_specs, check_vma=False
    )
```

```python
import functools

import jax
import jax.numpy as jnp
from jax import lax
from jax.experimental import pallas as pl
from jax.experimental.pallas import tpu as pltpu
from jax.sharding import Mesh, PartitionSpec as P

HQ = 32
KVH = 16
HD = 128
CAP = 50
SCALAR = 144
KV = ("kx", "kc")
TQ = 1024


def block_kernel(sc_ref, q_ref, k_ref, v_ref, l_ref, acc_ref, l_out, acc_out, *, slot, rows):
    tq = q_ref.shape[0]
    tk = k_ref.shape[0]
    span = min(tq, rows)
    row_first = sc_ref[0] + (pl.program_id(0) * tq) % rows
    row_last = row_first + span - 1
    key_first = sc_ref[1 + slot]
    key_last = key_first + tk - 1

    def update(masked):
        raw = lax.dot_general(
            q_ref[...], k_ref[...], (((1,), (1,)), ((), ())), preferred_element_type=jnp.float32
        )
        prob = jnp.exp(CAP * jnp.tanh(raw * (SCALAR ** (-0.5) / CAP)))
        if masked:
            q_pos = row_first + (lax.broadcasted_iota(jnp.int32, (tq, tk), 0) & (span - 1))
            k_pos = key_first + lax.broadcasted_iota(jnp.int32, (tq, tk), 1)
            prob = jnp.where(k_pos <= q_pos, prob, 0.0)
        l_out[...] = l_ref[...] + jnp.sum(prob, axis=1, keepdims=True)
        acc_out[...] = acc_ref[...] + jnp.dot(
            prob.astype(jnp.bfloat16), v_ref[...], preferred_element_type=jnp.float32
        )

    @pl.when(key_first > row_last)
    def _skip():
        l_out[...] = l_ref[...]
        acc_out[...] = acc_ref[...]

    @pl.when(key_last <= row_first)
    def _full():
        update(False)

    @pl.when(jnp.logical_and(key_first <= row_last, key_last > row_first))
    def _diagonal():
        update(True)


def attend_kernel(scalars, slot, rows, q, block, total, summed):
    n_q, hd = q.shape
    n_k = block.shape[1]
    tq = min(TQ, n_q)
    row = lambda i, sc: (i, 0)
    grid_spec = pltpu.PrefetchScalarGridSpec(
        num_scalar_prefetch=1,
        grid=(n_q // tq,),
        in_specs=[
            pl.BlockSpec((tq, hd), row),
            pl.BlockSpec((None, n_k, hd), lambda i, sc: (0, 0, 0)),
            pl.BlockSpec((None, n_k, hd), lambda i, sc: (1, 0, 0)),
            pl.BlockSpec((tq, 1), row),
            pl.BlockSpec((tq, hd), row),
        ],
        out_specs=[
            pl.BlockSpec((tq, 1), row),
            pl.BlockSpec((tq, hd), row),
        ],
    )
    return pl.pallas_call(
        functools.partial(block_kernel, slot=slot, rows=rows),
        grid_spec=grid_spec,
        out_shape=(
            jax.ShapeDtypeStruct(total.shape, jnp.float32),
            jax.ShapeDtypeStruct(summed.shape, jnp.float32),
        ),
        input_output_aliases={4: 0, 5: 1},
        cost_estimate=pl.CostEstimate(
            flops=4 * n_q * n_k * hd,
            transcendentals=2 * n_q * n_k,
            bytes_accessed=2 * (n_q + 2 * n_k) * hd + 8 * n_q * (hd + 1),
        ),
    )(scalars, q, block, block, total, summed)


def by_heads(queries, keys, values, row_first):
    n_kv = lax.axis_size(KV)
    me = lax.axis_index(KV)
    group = HQ // KVH
    rows_dev = queries.shape[0]
    key_dev = keys.shape[0]
    kv_local = keys.shape[1] // (n_kv * HD)
    kv_feat = kv_local * HD
    n_q = kv_local * group * rows_dev
    q_block = queries.reshape(rows_dev, kv_local * group, HD).transpose(1, 0, 2).reshape(n_q, HD)
    total = jnp.zeros((n_q, 1), jnp.float32)
    summed = jnp.zeros((n_q, HD), jnp.float32)
    sources = me ^ jnp.arange(n_kv, dtype=jnp.int32)
    scalars = jnp.concatenate([row_first[None], sources * key_dev]).astype(jnp.int32)
    for shift in range(n_kv):
        dest = me ^ shift
        src = dest
        block = jnp.stack(
            (
                lax.dynamic_slice_in_dim(keys, dest * kv_feat, kv_feat, 1),
                lax.dynamic_slice_in_dim(values, dest * kv_feat, kv_feat, 1),
            ),
            axis=0,
        )
        if shift:
            block = lax.ppermute(block, KV, [(j, j ^ shift) for j in range(n_kv)])
        total, summed = attend_kernel(scalars, shift, rows_dev, q_block, block, total, summed)
    mixed = (summed / total).astype(jnp.bfloat16)
    return mixed.reshape(kv_local * group, rows_dev, HD).transpose(1, 0, 2).reshape(rows_dev, n_q // rows_dev * HD)


def per_device(slab_start, queries, keys, values, out_weight):
    rows_dev = queries.shape[0]
    row_first = slab_start[0] + lax.axis_index("pb") * rows_dev
    attended = by_heads(queries, keys, values, row_first)
    partial = jnp.dot(attended, out_weight, preferred_element_type=jnp.float32)
    n_chip = lax.axis_size("kx")
    n_core = lax.axis_size("kc")
    partial = partial.reshape(n_chip, n_core, rows_dev // (n_chip * n_core), partial.shape[1])
    core = lax.axis_index("kc")
    mine = lax.dynamic_index_in_dim(partial, core, 1, keepdims=False)
    theirs = lax.dynamic_index_in_dim(partial, 1 - core, 1, keepdims=False)
    on_chip = mine + lax.ppermute(theirs, "kc", [(0, 1), (1, 0)])
    parts = lax.all_to_all(
        on_chip.astype(jnp.bfloat16), "kx", split_axis=0, concat_axis=0, tiled=True
    )
    return jnp.sum(parts.astype(jnp.float32), axis=0)


def solution(mesh):
    n_pb, n_kv = mesh.devices.shape
    split = Mesh(mesh.devices.reshape(n_pb, n_kv // 2, 2), ("pb", "kx", "kc"))
    in_specs = (P(), P("pb", KV), P(KV, None), P(KV, None), P(KV, None))
    out_specs = P(("pb",) + KV, None)
    return jax.shard_map(
        per_device, mesh=split, in_specs=in_specs, out_specs=out_specs, check_vma=False
    )
```
